512 devices in a mesh: pool: 64 (over y, z), tensor: 8 (over x, core).
Axes of the slice: x: 4, y: 4, z: 16, core: 2. Of those that a mesh axis runs over, the one named last changes fastest.
Arguments:
- queries: bfloat16 [8192, 4096], P(('pool', 'tensor')), may hold values from -6 to 6
- incoming_keys: bfloat16 [8192, 2048], P(('pool', 'tensor')), may hold values from -6 to 6
- incoming_values: bfloat16 [8192, 2048], P(('pool', 'tensor')), may hold values from -6 to 6
- cached_key_pages: bfloat16 [1024, 128, 2048], P('pool', None, 'tensor'), may hold values from -6 to 6
- cached_value_pages: bfloat16 [1024, 128, 2048], P('pool', None, 'tensor'), may hold values from -6 to 6
- page_table: int32 [64, 64], replicated, may hold values from -1 to 1023, as said below
- lengths: int32 [64], replicated, may hold values from 1 to 8192, as said below
Outputs:
- attended: bfloat16 [8192, 4096], P(('pool', 'tensor'))
The draws below stay inside these ranges and needn't reach their ends.
Inputs may be any that keep to these rules, and one draw needn't show every extreme that they name: Request r has ceil(lengths[r] / 128) pages; for j below that, page_table[r, j] is the slot of its page j, a slot g of pool device g // 16, which is one of r, r + 1, ..., r + 3 counted modulo 64. No slot holds two pages. All other entries are -1. `lengths`: some request has exactly 8192 cached tokens.
All inputs are finite; a program needn't handle non-finite values.
Results may differ from the reference program's by a relative error of at most 0.008.
Values may be sent and summed in bfloat16 or wider, within the bound.
No kernel may reach another device: no remote copies, remote signals or barrier semaphores. Data moves between devices by JAX's collectives and lax.ppermute only.
A program may use at most 64 MiB of HBM per device.

```python
import jax
import jax.numpy as jnp
from jax import lax

QUERY_HEADS = 16
KEY_VALUE_HEADS = 8
HEAD_SIZE = 256
REQUEST_TOKENS = 128
PAGE_TOKENS = 128
SPAN = 4
POOL_PAGE_SLOTS = 16
REQUEST_COUNT = 64
NEW_TOKEN_COUNT = 8192
TOTAL_SLOTS = 1024
MAXP = 64
N_POOL = 64


def draw_layout(key):
    folded = jax.random.fold_in(key, 7)
    star_key, which_key, fill_key, alive_key, order_key, length_key = jax.random.split(folded, 6)
    slot_total = REQUEST_COUNT * POOL_PAGE_SLOTS
    holder = jnp.arange(slot_total, dtype=jnp.int32) // POOL_PAGE_SLOTS
    position = jnp.arange(slot_total, dtype=jnp.int32) % POOL_PAGE_SLOTS
    longest = jax.random.randint(star_key, (), 0, REQUEST_COUNT).astype(jnp.int32)
    distance = jax.random.randint(which_key, (slot_total,), 0, SPAN).astype(jnp.int32)
    fill_level = jax.random.randint(fill_key, (REQUEST_COUNT,), 3, 11)
    alive = jax.random.randint(alive_key, (slot_total,), 0, 10) < fill_level[holder]
    alive = alive | (position == POOL_PAGE_SLOTS - 1) | (position == 0)
    distance = jnp.where(position == 0, 0, distance)
    offset = (holder - longest) % REQUEST_COUNT
    in_block = offset < SPAN
    next_holder = offset == SPAN
    special = next_holder & (position >= 1) & (position < SPAN)
    distance = jnp.where(special, SPAN - position, distance)
    alive = alive | special
    distance = jnp.where(in_block, offset, distance)
    alive = alive | in_block
    slot_owner = jnp.where(alive, (holder - distance) % REQUEST_COUNT, REQUEST_COUNT).astype(jnp.int32)
    priority = jax.random.permutation(order_key, slot_total).astype(jnp.int32)
    same_owner = slot_owner[:, None] == slot_owner[None, :]
    before = priority[None, :] < priority[:, None]
    page_rank = jnp.sum(same_owner & before, axis=1).astype(jnp.int32)
    table_out = jnp.full((REQUEST_COUNT + 1, MAXP), -1, jnp.int32)
    table_out = table_out.at[slot_owner, page_rank].set(jnp.arange(slot_total, dtype=jnp.int32), mode='drop')[:REQUEST_COUNT]
    page_count = jnp.sum(table_out >= 0, axis=1).astype(jnp.int32)
    last_fill = jax.random.randint(length_key, (REQUEST_COUNT,), 1, PAGE_TOKENS + 1).astype(jnp.int32)
    length_out = (page_count - 1) * PAGE_TOKENS + last_fill
    length_out = jnp.where(jnp.arange(REQUEST_COUNT, dtype=jnp.int32) == longest, MAXP * PAGE_TOKENS, length_out)
    return (table_out, length_out.astype(jnp.int32))


def draw_page_table(key, part):
    return draw_layout(key)[0]


def draw_lengths(key, part):
    return draw_layout(key)[1]


def block_scale(key, extent, pieces, least, largest):
    factor_of = 1.0
    for dim, blocks in pieces:
        steps = jax.random.uniform(jax.random.fold_in(jax.random.fold_in(key, 6), dim), (blocks,), jnp.float32, least / len(pieces), largest / len(pieces))
        factor_of = factor_of * jnp.repeat(jnp.exp(steps), extent[dim] // blocks).reshape((-1,) + (1,) * (len(extent) - 1 - dim))
    return factor_of


def noise(stream_key, extent, width, limit, pieces=(), held_as=jnp.bfloat16):
    entries = jax.random.normal(stream_key, extent, jnp.float32) * width
    if len(pieces) > 0:
        entries = block_scale(stream_key, extent, pieces, -0.22, 0.18) * entries
    return jnp.clip(entries, min=-limit, max=limit).astype(held_as)


def setup_inputs(seed: int = 0) -> dict:
    arg_keys = jax.random.split(jax.random.key(seed), 8)
    queries = noise(arg_keys[0], (NEW_TOKEN_COUNT, QUERY_HEADS * HEAD_SIZE), 1.0, 6.0, ((0, 512),))
    incoming_keys = noise(arg_keys[1], (NEW_TOKEN_COUNT, KEY_VALUE_HEADS * HEAD_SIZE), 1.0, 6.0, ((0, 512),))
    incoming_values = noise(arg_keys[2], (NEW_TOKEN_COUNT, KEY_VALUE_HEADS * HEAD_SIZE), 1.0, 6.0, ((0, 512),))
    cached_key_pages = noise(arg_keys[3], (TOTAL_SLOTS, PAGE_TOKENS, KEY_VALUE_HEADS * HEAD_SIZE), 1.0, 6.0, ((0, 64), (2, 8)))
    cached_value_pages = noise(arg_keys[4], (TOTAL_SLOTS, PAGE_TOKENS, KEY_VALUE_HEADS * HEAD_SIZE), 1.0, 6.0, ((0, 64), (2, 8)))
    page_table = draw_page_table(jax.random.fold_in(arg_keys[7], 71), 0)
    lengths = draw_lengths(jax.random.fold_in(arg_keys[7], 71), 0)
    return dict(queries=queries, incoming_keys=incoming_keys, incoming_values=incoming_values, cached_key_pages=cached_key_pages, cached_value_pages=cached_value_pages, page_table=page_table, lengths=lengths)


SOFTCAP = 50.0


def capped(scores, visible):
    capped_scores = SOFTCAP * jnp.tanh(scores / SOFTCAP)
    return jnp.where(visible, jnp.exp(capped_scores), 0.0).astype(jnp.bfloat16)


def reference(queries, incoming_keys, incoming_values, cached_key_pages, cached_value_pages, page_table, lengths):
    query_group_width = QUERY_HEADS // KEY_VALUE_HEADS
    score_scale = HEAD_SIZE ** -0.5
    query_layout_grid = queries.reshape(REQUEST_COUNT, REQUEST_TOKENS, KEY_VALUE_HEADS, query_group_width, HEAD_SIZE).astype(jnp.float32)
    fresh_key_rows = incoming_keys.reshape(REQUEST_COUNT, REQUEST_TOKENS, KEY_VALUE_HEADS, HEAD_SIZE).astype(jnp.float32)
    fresh_value_rows = incoming_values.reshape(REQUEST_COUNT, REQUEST_TOKENS, KEY_VALUE_HEADS, HEAD_SIZE).astype(jnp.float32)
    causal = jnp.arange(REQUEST_TOKENS)[None, :] <= jnp.arange(REQUEST_TOKENS)[:, None]
    own_scores = jnp.einsum('rqgah,rkgh->rgaqk', query_layout_grid, fresh_key_rows) * score_scale
    own_weights = capped(own_scores, causal).astype(jnp.float32)
    own_numer = jnp.einsum('rgaqk,rkgh->rqgah', own_weights, fresh_value_rows)
    own_total = jnp.sum(own_weights, axis=-1)

    flat_table = page_table.reshape(-1)
    request_ids = jnp.repeat(jnp.arange(REQUEST_COUNT, dtype=jnp.int32), MAXP)
    page_ids = jnp.tile(jnp.arange(MAXP, dtype=jnp.int32), REQUEST_COUNT)
    target = jnp.where(flat_table >= 0, flat_table, TOTAL_SLOTS).astype(jnp.int32)
    slot_owner = jnp.full((TOTAL_SLOTS,), REQUEST_COUNT, jnp.int32).at[target].set(request_ids, mode='drop')
    slot_page = jnp.zeros((TOTAL_SLOTS,), jnp.int32).at[target].set(page_ids, mode='drop')
    slot_limit = jnp.where(slot_owner < REQUEST_COUNT, jnp.take(lengths, jnp.minimum(slot_owner, REQUEST_COUNT - 1)), 0).astype(jnp.int32)

    def one_block(running, input_arrays):
        key_page_block, value_page_block, owner_block, page_block, limit_block = input_arrays
        query_pick = jnp.take(query_layout_grid, jnp.minimum(owner_block, REQUEST_COUNT - 1), axis=0)
        key_layout_grid = key_page_block.reshape(POOL_PAGE_SLOTS, PAGE_TOKENS, KEY_VALUE_HEADS, HEAD_SIZE).astype(jnp.float32)
        value_layout_grid = value_page_block.reshape(POOL_PAGE_SLOTS, PAGE_TOKENS, KEY_VALUE_HEADS, HEAD_SIZE).astype(jnp.float32)
        scores = jnp.einsum('bqgah,bkgh->bgaqk', query_pick, key_layout_grid) * score_scale
        position = page_block[:, None] * PAGE_TOKENS + jnp.arange(PAGE_TOKENS, dtype=jnp.int32)[None, :]
        visible = position < limit_block[:, None]
        weights = capped(scores, visible[:, None, None, None, :]).astype(jnp.float32)
        numer = jnp.einsum('bgaqk,bkgh->bqgah', weights, value_layout_grid)
        totals = jnp.sum(weights, axis=-1)
        numer_acc, total_acc = running
        return (numer_acc.at[owner_block].add(numer), total_acc.at[owner_block].add(totals)), None

    start_offset = (jnp.zeros((REQUEST_COUNT + 1, REQUEST_TOKENS, KEY_VALUE_HEADS, query_group_width, HEAD_SIZE), jnp.float32),
             jnp.zeros((REQUEST_COUNT + 1, KEY_VALUE_HEADS, query_group_width, REQUEST_TOKENS), jnp.float32))
    input_arrays = (cached_key_pages.reshape(N_POOL, POOL_PAGE_SLOTS, PAGE_TOKENS, KEY_VALUE_HEADS * HEAD_SIZE),
              cached_value_pages.reshape(N_POOL, POOL_PAGE_SLOTS, PAGE_TOKENS, KEY_VALUE_HEADS * HEAD_SIZE),
              slot_owner.reshape(N_POOL, POOL_PAGE_SLOTS),
              slot_page.reshape(N_POOL, POOL_PAGE_SLOTS),
              slot_limit.reshape(N_POOL, POOL_PAGE_SLOTS))
    (numer_acc, total_acc), _ = lax.scan(one_block, start_offset, input_arrays)
    numerator = numer_acc[:REQUEST_COUNT] + own_numer
    totals = jnp.transpose(total_acc[:REQUEST_COUNT] + own_total, (0, 3, 1, 2))
    attended = numerator / totals[..., None]
    return attended.reshape(NEW_TOKEN_COUNT, QUERY_HEADS * HEAD_SIZE).astype(jnp.bfloat16)
```

```python
import functools

import jax
import jax.numpy as jnp
from jax import lax
from jax.experimental import pallas as pl
from jax.experimental.pallas import tpu as pltpu
from jax.sharding import PartitionSpec as P

QUERY_HEADS = 16
KEY_VALUE_HEADS = 8
HEAD_SIZE = 256
SPAN = 4

SOFTCAP = 50.0
SCORE_SCALE = HEAD_SIZE ** (-0.5)


def shifted(block, axis, distance):
    devices = range(lax.axis_size(axis))
    route = [((i - distance) % len(devices), i) for i in devices]
    return lax.ppermute(block, axis, route)


def _attend_kernel(ds, with_own, meta_ref, *refs):
    nq = len(ds)
    q_refs = refs[:nq]
    kp_ref, vp_ref = refs[nq], refs[nq + 1]
    rest = refs[nq + 2:]
    if with_own:
        kn_ref, vn_ref = rest[0], rest[1]
        rest = rest[2:]
    out_ref = rest[0]
    rows = q_refs[0].shape[0]
    slots, page_len, kv_width = kp_ref.shape
    kv_local = kv_width // HEAD_SIZE
    group = QUERY_HEADS // KEY_VALUE_HEADS
    out_ref[...] = jnp.zeros(out_ref.shape, jnp.float32)
    ones = jnp.ones((8, page_len), jnp.bfloat16)

    def add_block(i, q_ref, k, v, visible):
        for g in range(kv_local):
            kg = k[:, g * HEAD_SIZE:(g + 1) * HEAD_SIZE]
            vg = v[:, g * HEAD_SIZE:(g + 1) * HEAD_SIZE]
            for a in range(group):
                h = g * group + a
                col = h * HEAD_SIZE
                q = q_ref[:, col:col + HEAD_SIZE]
                s = lax.dot_general(
                    q, kg, (((1,), (1,)), ((), ())), preferred_element_type=jnp.float32
                ) * SCORE_SCALE
                w = jnp.where(visible, jnp.exp(SOFTCAP * jnp.tanh(s / SOFTCAP)), 0.0).astype(
                    jnp.bfloat16
                )
                out_ref[i, :rows, col:col + HEAD_SIZE] += jnp.dot(
                    w, vg, preferred_element_type=jnp.float32
                )
                t = lax.dot_general(
                    ones, w, (((1,), (1,)), ((), ())), preferred_element_type=jnp.float32
                )
                out_ref[i, rows:rows + 8, h * rows:(h + 1) * rows] += t

    key_pos = lax.broadcasted_iota(jnp.int32, (rows, page_len), 1)
    if with_own:
        q_pos = lax.broadcasted_iota(jnp.int32, (rows, page_len), 0)
        add_block(ds.index(0), q_refs[ds.index(0)], kn_ref[...], vn_ref[...], key_pos <= q_pos)

    def slot(s, carry):
        d = meta_ref[0, s]
        lim = meta_ref[1, s]
        for i, dd in enumerate(ds):
            @pl.when((d == dd) & (lim > 0))
            def _():
                add_block(i, q_refs[i], kp_ref[s], vp_ref[s], key_pos < lim)

        return carry

    lax.fori_loop(0, slots, slot, 0)


def attend(ds, meta, qs, kp, vp, kn=None, vn=None):
    with_own = kn is not None
    rows, width = qs[0].shape
    slots, page_len, kv_width = kp.shape
    args = [meta, *qs, kp, vp] + ([kn, vn] if with_own else [])
    blocks = slots + (1 if with_own else 0)
    heads = width // HEAD_SIZE
    flops = blocks * heads * rows * page_len * HEAD_SIZE * 4
    cost = pl.CostEstimate(
        flops=flops,
        transcendentals=blocks * heads * rows * page_len * 2,
        bytes_accessed=sum(int(x.size) * x.dtype.itemsize for x in args)
        + len(ds) * (rows + 8) * width * 4,
    )
    return pl.pallas_call(
        functools.partial(_attend_kernel, tuple(ds), with_own),
        out_shape=jax.ShapeDtypeStruct((len(ds), rows + 8, width), jnp.float32),
        in_specs=[pl.BlockSpec(memory_space=pltpu.SMEM)]
        + [pl.BlockSpec(memory_space=pltpu.VMEM)] * (len(args) - 1),
        out_specs=pl.BlockSpec(memory_space=pltpu.VMEM),
        cost_estimate=cost,
    )(*args)


def on_device(
    queries,
    incoming_keys,
    incoming_values,
    cached_key_pages,
    cached_value_pages,
    page_table,
    lengths,
):
    tensor_size = lax.axis_size("tensor")
    n_tok = queries.shape[0]
    q_width = queries.shape[1] // tensor_size
    kv_width = incoming_keys.shape[1] // tensor_size
    packed = jnp.concatenate(
        [
            queries.reshape(n_tok, tensor_size, q_width),
            incoming_keys.reshape(n_tok, tensor_size, kv_width),
            incoming_values.reshape(n_tok, tensor_size, kv_width),
        ],
        axis=2,
    )
    mixed = lax.all_to_all(packed, "tensor", split_axis=1, concat_axis=0, tiled=True)
    rows = mixed.shape[0]
    mixed = mixed.reshape(rows, q_width + 2 * kv_width)
    q_own = mixed[:, :q_width]
    k_new = mixed[:, q_width:q_width + kv_width]
    v_new = mixed[:, q_width + kv_width:]

    received = [q_own] + [shifted(q_own, "pool", offset) for offset in range(1, SPAN)]

    pool_size = lax.axis_size("pool")
    holder = lax.axis_index("pool")
    slots_dev = cached_key_pages.shape[0]
    page_len = cached_key_pages.shape[1]
    owners = (holder - jnp.arange(SPAN, dtype=jnp.int32)) % pool_size
    table_rows = jnp.take(page_table, owners, axis=0)
    global_slot = holder * slots_dev + jnp.arange(slots_dev, dtype=jnp.int32)
    matches = table_rows[:, :, None] == global_slot[None, None, :]
    owner_hot = jnp.any(matches, axis=1)
    page_index = jnp.sum(
        jnp.where(matches, jnp.arange(table_rows.shape[1], dtype=jnp.int32)[None, :, None], 0),
        axis=(0, 1),
    )
    distance = jnp.sum(jnp.where(owner_hot, jnp.arange(SPAN, dtype=jnp.int32)[:, None], 0), axis=0)
    owner_len = jnp.take(lengths, owners)
    slot_len = jnp.sum(jnp.where(owner_hot, owner_len[:, None], 0), axis=0)
    limit = jnp.clip(slot_len - page_index * page_len, 0, page_len)
    meta = jnp.stack([distance, limit]).astype(jnp.int32)

    acc = attend(
        list(range(SPAN)), meta, received, cached_key_pages, cached_value_pages, k_new, v_new
    )
    total = acc[0]
    for offset in range(1, SPAN):
        total = total + shifted(acc[offset], "pool", -offset)
    heads = q_width // HEAD_SIZE
    numerator = total[:rows].reshape(rows, heads, HEAD_SIZE)
    totals = total[rows, : heads * rows].reshape(heads, rows)
    attended = numerator / jnp.transpose(totals)[:, :, None]
    attended = attended.reshape(rows, q_width).astype(jnp.bfloat16)
    return lax.all_to_all(attended, "tensor", split_axis=0, concat_axis=1, tiled=True)


def solution(mesh):
    placed = (
        P(("pool", "tensor"), None),
        P(("pool", "tensor"), None),
        P(("pool", "tensor"), None),
        P("pool", None, "tensor"),
        P("pool", None, "tensor"),
        P(),
        P(),
    )
    return jax.shard_map(
        on_device,
        mesh=mesh,
        in_specs=placed,
        out_specs=P(("pool", "tensor"), None),
        check_vma=False,
    )
```

```python
import functools

import jax
import jax.numpy as jnp
from jax import lax
from jax.experimental import pallas as pl
from jax.experimental.pallas import tpu as pltpu
from jax.sharding import PartitionSpec as P

QUERY_HEADS = 16
KEY_VALUE_HEADS = 8
HEAD_SIZE = 256
SPAN = 4

SOFTCAP = 50.0
SCORE_SCALE = HEAD_SIZE ** (-0.5)


def shifted(block, axis, distance):
    devices = range(lax.axis_size(axis))
    route = [((i - distance) % len(devices), i) for i in devices]
    return lax.ppermute(block, axis, route)


def _attend_kernel(ds, with_own, meta_ref, *refs):
    nq = len(ds)
    q_refs = refs[:nq]
    kp_ref, vp_ref = refs[nq], refs[nq + 1]
    rest = refs[nq + 2:]
    if with_own:
        kn_ref, vn_ref = rest[0], rest[1]
        rest = rest[2:]
    out_ref = rest[0]
    rows = q_refs[0].shape[0]
    slots, page_len, kv_width = kp_ref.shape
    kv_local = kv_width // HEAD_SIZE
    group = QUERY_HEADS // KEY_VALUE_HEADS
    out_ref[...] = jnp.zeros(out_ref.shape, jnp.float32)
    ones = jnp.ones((8, page_len), jnp.bfloat16)

    def add_block(i, q_ref, k, v, visible):
        for g in range(kv_local):
            kg = k[:, g * HEAD_SIZE:(g + 1) * HEAD_SIZE]
            vg = v[:, g * HEAD_SIZE:(g + 1) * HEAD_SIZE]
            for a in range(group):
                h = g * group + a
                col = h * HEAD_SIZE
                q = q_ref[:, col:col + HEAD_SIZE]
                s = lax.dot_general(
                    q, kg, (((1,), (1,)), ((), ())), preferred_element_type=jnp.float32
                ) * SCORE_SCALE
                w = jnp.where(visible, jnp.exp(SOFTCAP * jnp.tanh(s / SOFTCAP)), 0.0).astype(
                    jnp.bfloat16
                )
                out_ref[i, :rows, col:col + HEAD_SIZE] += jnp.dot(
                    w, vg, preferred_element_type=jnp.float32
                )
                t = lax.dot_general(
                    ones, w, (((1,), (1,)), ((), ())), preferred_element_type=jnp.float32
                )
                out_ref[i, rows:rows + 8, h * rows:(h + 1) * rows] += t

    key_pos = lax.broadcasted_iota(jnp.int32, (rows, page_len), 1)
    if with_own:
        q_pos = lax.broadcasted_iota(jnp.int32, (rows, page_len), 0)
        add_block(ds.index(0), q_refs[ds.index(0)], kn_ref[...], vn_ref[...], key_pos <= q_pos)

    def slot(s, carry):
        d = meta_ref[0, s]
        lim = meta_ref[1, s]
        for i, dd in enumerate(ds):
            @pl.when((d == dd) & (lim > 0))
            def _():
                add_block(i, q_refs[i], kp_ref[s], vp_ref[s], key_pos < lim)

        return carry

    lax.fori_loop(0, slots, slot, 0)


def attend(ds, meta, qs, kp, vp, kn=None, vn=None):
    with_own = kn is not None
    rows, width = qs[0].shape
    slots, page_len, kv_width = kp.shape
    args = [meta, *qs, kp, vp] + ([kn, vn] if with_own else [])
    blocks = slots + (1 if with_own else 0)
    heads = width // HEAD_SIZE
    flops = blocks * heads * rows * page_len * HEAD_SIZE * 4
    cost = pl.CostEstimate(
        flops=flops,
        transcendentals=blocks * heads * rows * page_len * 2,
        bytes_accessed=sum(int(x.size) * x.dtype.itemsize for x in args)
        + len(ds) * (rows + 8) * width * 4,
    )
    return pl.pallas_call(
        functools.partial(_attend_kernel, tuple(ds), with_own),
        out_shape=jax.ShapeDtypeStruct((len(ds), rows + 8, width), jnp.float32),
        in_specs=[pl.BlockSpec(memory_space=pltpu.SMEM)]
        + [pl.BlockSpec(memory_space=pltpu.VMEM)] * (len(args) - 1),
        out_specs=pl.BlockSpec(memory_space=pltpu.VMEM),
        cost_estimate=cost,
    )(*args)


def on_device(
    queries,
    incoming_keys,
    incoming_values,
    cached_key_pages,
    cached_value_pages,
    page_table,
    lengths,
):
    tensor_size = lax.axis_size("tensor")
    n_tok = queries.shape[0]
    q_width = queries.shape[1] // tensor_size
    kv_width = incoming_keys.shape[1] // tensor_size
    packed = jnp.concatenate(
        [
            queries.reshape(n_tok, tensor_size, q_width),
            incoming_keys.reshape(n_tok, tensor_size, kv_width),
            incoming_values.reshape(n_tok, tensor_size, kv_width),
        ],
        axis=2,
    )
    mixed = lax.all_to_all(packed, "tensor", split_axis=1, concat_axis=0, tiled=True)
    rows = mixed.shape[0]
    mixed = mixed.reshape(rows, q_width + 2 * kv_width)
    q_own = mixed[:, :q_width]
    k_new = mixed[:, q_width:q_width + kv_width]
    v_new = mixed[:, q_width + kv_width:]

    received = [q_own]
    for offset in range(1, SPAN):
        received.append(shifted(received[-1], "pool", 1))

    pool_size = lax.axis_size("pool")
    holder = lax.axis_index("pool")
    slots_dev = cached_key_pages.shape[0]
    page_len = cached_key_pages.shape[1]
    owners = (holder - jnp.arange(SPAN, dtype=jnp.int32)) % pool_size
    table_rows = jnp.take(page_table, owners, axis=0)
    global_slot = holder * slots_dev + jnp.arange(slots_dev, dtype=jnp.int32)
    matches = table_rows[:, :, None] == global_slot[None, None, :]
    owner_hot = jnp.any(matches, axis=1)
    page_index = jnp.sum(
        jnp.where(matches, jnp.arange(table_rows.shape[1], dtype=jnp.int32)[None, :, None], 0),
        axis=(0, 1),
    )
    distance = jnp.sum(jnp.where(owner_hot, jnp.arange(SPAN, dtype=jnp.int32)[:, None], 0), axis=0)
    owner_len = jnp.take(lengths, owners)
    slot_len = jnp.sum(jnp.where(owner_hot, owner_len[:, None], 0), axis=0)
    limit = jnp.clip(slot_len - page_index * page_len, 0, page_len)
    meta = jnp.stack([distance, limit]).astype(jnp.int32)

    parts = [
        attend([0], meta, received[:1], cached_key_pages, cached_value_pages, k_new, v_new)[0]
    ]
    for offset in range(1, SPAN):
        parts.append(
            attend([offset], meta, received[offset : offset + 1], cached_key_pages, cached_value_pages)[0]
        )
    total = parts[SPAN - 1]
    for offset in range(SPAN - 2, -1, -1):
        total = parts[offset] + shifted(total, "pool", -1)
    heads = q_width // HEAD_SIZE
    numerator = total[:rows].reshape(rows, heads, HEAD_SIZE)
    totals = total[rows, : heads * rows].reshape(heads, rows)
    attended = numerator / jnp.transpose(totals)[:, :, None]
    attended = attended.reshape(rows, q_width).astype(jnp.bfloat16)
    return lax.all_to_all(attended, "tensor", split_axis=0, concat_axis=1, tiled=True)


def solution(mesh):
    placed = (
        P(("pool", "tensor"), None),
        P(("pool", "tensor"), None),
        P(("pool", "tensor"), None),
        P("pool", None, "tensor"),
        P("pool", None, "tensor"),
        P(),
        P(),
    )
    return jax.shard_map(
        on_device,
        mesh=mesh,
        in_specs=placed,
        out_specs=P(("pool", "tensor"), None),
        check_vma=False,
    )
```

```python
import functools

import jax
import jax.numpy as jnp
from jax import lax
from jax.experimental import pallas as pl
from jax.experimental.pallas import tpu as pltpu
from jax.sharding import PartitionSpec as P

QUERY_HEADS = 16
KEY_VALUE_HEADS = 8
HEAD_SIZE = 256
SPAN = 4

SOFTCAP = 50.0
SCORE_SCALE = HEAD_SIZE ** (-0.5)


def shifted(block, axis, distance):
    devices = range(lax.axis_size(axis))
    route = [((i - distance) % len(devices), i) for i in devices]
    return lax.ppermute(block, axis, route)


def _attend_kernel(ds, with_own, meta_ref, *refs):
    nq = len(ds)
    q_refs = refs[:nq]
    kp_ref, vp_ref = refs[nq], refs[nq + 1]
    rest = refs[nq + 2:]
    if with_own:
        kn_ref, vn_ref = rest[0], rest[1]
        rest = rest[2:]
    out_ref = rest[0]
    rows = q_refs[0].shape[0]
    slots, page_len, kv_width = kp_ref.shape
    kv_local = kv_width // HEAD_SIZE
    group = QUERY_HEADS // KEY_VALUE_HEADS
    out_ref[...] = jnp.zeros(out_ref.shape, jnp.float32)
    ones = jnp.ones((8, page_len), jnp.bfloat16)

    def add_block(i, q_ref, k, v, visible):
        for g in range(kv_local):
            kg = k[:, g * HEAD_SIZE:(g + 1) * HEAD_SIZE]
            vg = v[:, g * HEAD_SIZE:(g + 1) * HEAD_SIZE]
            for a in range(group):
                h = g * group + a
                col = h * HEAD_SIZE
                q = q_ref[:, col:col + HEAD_SIZE]
                s = lax.dot_general(
                    q, kg, (((1,), (1,)), ((), ())), preferred_element_type=jnp.float32
                ) * SCORE_SCALE
                w = jnp.where(visible, jnp.exp(SOFTCAP * jnp.tanh(s / SOFTCAP)), 0.0).astype(
                    jnp.bfloat16
                )
                out_ref[i, :rows, col:col + HEAD_SIZE] += jnp.dot(
                    w, vg, preferred_element_type=jnp.float32
                )
                t = lax.dot_general(
                    ones, w, (((1,), (1,)), ((), ())), preferred_element_type=jnp.float32
                )
                out_ref[i, rows:rows + 8, h * rows:(h + 1) * rows] += t

    key_pos = lax.broadcasted_iota(jnp.int32, (rows, page_len), 1)
    if with_own:
        q_pos = lax.broadcasted_iota(jnp.int32, (rows, page_len), 0)
        add_block(ds.index(0), q_refs[ds.index(0)], kn_ref[...], vn_ref[...], key_pos <= q_pos)

    def slot(s, carry):
        d = meta_ref[0, s]
        lim = meta_ref[1, s]
        for i, dd in enumerate(ds):
            @pl.when((d == dd) & (lim > 0))
            def _():
                add_block(i, q_refs[i], kp_ref[s], vp_ref[s], key_pos < lim)

        return carry

    lax.fori_loop(0, slots, slot, 0)


def attend(ds, meta, qs, kp, vp, kn=None, vn=None):
    with_own = kn is not None
    rows, width = qs[0].shape
    slots, page_len, kv_width = kp.shape
    args = [meta, *qs, kp, vp] + ([kn, vn] if with_own else [])
    blocks = slots + (1 if with_own else 0)
    heads = width // HEAD_SIZE
    flops = blocks * heads * rows * page_len * HEAD_SIZE * 4
    cost = pl.CostEstimate(
        flops=flops,
        transcendentals=blocks * heads * rows * page_len * 2,
        bytes_accessed=sum(int(x.size) * x.dtype.itemsize for x in args)
        + len(ds) * (rows + 8) * width * 4,
    )
    return pl.pallas_call(
        functools.partial(_attend_kernel, tuple(ds), with_own),
        out_shape=jax.ShapeDtypeStruct((len(ds), rows + 8, width), jnp.float32),
        in_specs=[pl.BlockSpec(memory_space=pltpu.SMEM)]
        + [pl.BlockSpec(memory_space=pltpu.VMEM)] * (len(args) - 1),
        out_specs=pl.BlockSpec(memory_space=pltpu.VMEM),
        cost_estimate=cost,
    )(*args)


def on_device(
    queries,
    incoming_keys,
    incoming_values,
    cached_key_pages,
    cached_value_pages,
    page_table,
    lengths,
):
    tensor_size = lax.axis_size("tensor")
    n_tok = queries.shape[0]
    q_width = queries.shape[1] // tensor_size
    kv_width = incoming_keys.shape[1] // tensor_size
    packed = jnp.concatenate(
        [
            queries.reshape(n_tok, tensor_size, q_width),
            incoming_keys.reshape(n_tok, tensor_size, kv_width),
            incoming_values.reshape(n_tok, tensor_size, kv_width),
        ],
        axis=2,
    )
    mixed = lax.all_to_all(packed, "tensor", split_axis=1, concat_axis=0, tiled=True)
    rows = mixed.shape[0]
    mixed = mixed.reshape(rows, q_width + 2 * kv_width)
    q_own = mixed[:, :q_width]
    k_new = mixed[:, q_width:q_width + kv_width]
    v_new = mixed[:, q_width + kv_width:]

    pool_size = lax.axis_size("pool")
    holder = lax.axis_index("pool")
    slots_dev = cached_key_pages.shape[0]
    page_len = cached_key_pages.shape[1]
    owners = (holder - jnp.arange(SPAN, dtype=jnp.int32)) % pool_size
    table_rows = jnp.take(page_table, owners, axis=0)
    global_slot = holder * slots_dev + jnp.arange(slots_dev, dtype=jnp.int32)
    matches = table_rows[:, :, None] == global_slot[None, None, :]
    owner_hot = jnp.any(matches, axis=1)
    page_index = jnp.sum(
        jnp.where(matches, jnp.arange(table_rows.shape[1], dtype=jnp.int32)[None, :, None], 0),
        axis=(0, 1),
    )
    distance = jnp.sum(jnp.where(owner_hot, jnp.arange(SPAN, dtype=jnp.int32)[:, None], 0), axis=0)
    owner_len = jnp.take(lengths, owners)
    slot_len = jnp.sum(jnp.where(owner_hot, owner_len[:, None], 0), axis=0)
    limit = jnp.clip(slot_len - page_index * page_len, 0, page_len)
    meta = jnp.stack([distance, limit]).astype(jnp.int32)

    held = q_own
    parts = []
    for offset in range(SPAN):
        own = (k_new, v_new) if offset == 0 else ()
        part = attend([offset], meta, [held], cached_key_pages, cached_value_pages, *own)[0]
        if offset < SPAN - 1:
            held, part = lax.optimization_barrier((shifted(held, "pool", 1), part))
        parts.append(part)
    total = parts[SPAN - 1]
    for offset in range(SPAN - 2, -1, -1):
        total = parts[offset] + shifted(total, "pool", -1)
    heads = q_width // HEAD_SIZE
    numerator = total[:rows].reshape(rows, heads, HEAD_SIZE)
    totals = total[rows, : heads * rows].reshape(heads, rows)
    attended = numerator / jnp.transpose(totals)[:, :, None]
    attended = attended.reshape(rows, q_width).astype(jnp.bfloat16)
    return lax.all_to_all(attended, "tensor", split_axis=0, concat_axis=1, tiled=True)


def solution(mesh):
    placed = (
        P(("pool", "tensor"), None),
        P(("pool", "tensor"), None),
        P(("pool", "tensor"), None),
        P("pool", None, "tensor"),
        P("pool", None, "tensor"),
        P(),
        P(),
    )
    return jax.shard_map(
        on_device,
        mesh=mesh,
        in_specs=placed,
        out_specs=P(("pool", "tensor"), None),
        check_vma=False,
    )
```

```python
import functools

import jax
import jax.numpy as jnp
from jax import lax
from jax.experimental import pallas as pl
from jax.experimental.pallas import tpu as pltpu
from jax.sharding import PartitionSpec as P

QUERY_HEADS = 16
KEY_VALUE_HEADS = 8
HEAD_SIZE = 256
SPAN = 4

SOFTCAP = 50.0
SCORE_SCALE = HEAD_SIZE ** (-0.5)


def shifted(block, axis, distance):
    devices = range(lax.axis_size(axis))
    route = [((i - distance) % len(devices), i) for i in devices]
    return lax.ppermute(block, axis, route)


def _attend_kernel(ds, with_own, meta_ref, *refs):
    nq = len(ds)
    q_refs = refs[:nq]
    kp_ref, vp_ref = refs[nq], refs[nq + 1]
    rest = refs[nq + 2:]
    if with_own:
        kn_ref, vn_ref = rest[0], rest[1]
        rest = rest[2:]
    out_ref = rest[0]
    rows = q_refs[0].shape[0]
    slots, page_len, kv_width = kp_ref.shape
    kv_local = kv_width // HEAD_SIZE
    group = QUERY_HEADS // KEY_VALUE_HEADS
    out_ref[...] = jnp.zeros(out_ref.shape, jnp.float32)
    ones = jnp.ones((8, page_len), jnp.bfloat16)

    def add_block(i, q_ref, k, v, visible):
        for g in range(kv_local):
            kg = k[:, g * HEAD_SIZE:(g + 1) * HEAD_SIZE]
            vg = v[:, g * HEAD_SIZE:(g + 1) * HEAD_SIZE]
            for a in range(group):
                h = g * group + a
                col = h * HEAD_SIZE
                q = q_ref[:, col:col + HEAD_SIZE]
                s = lax.dot_general(
                    q, kg, (((1,), (1,)), ((), ())), preferred_element_type=jnp.float32
                ) * SCORE_SCALE
                w = jnp.where(visible, jnp.exp(SOFTCAP * jnp.tanh(s / SOFTCAP)), 0.0).astype(
                    jnp.bfloat16
                )
                out_ref[i, :rows, col:col + HEAD_SIZE] += jnp.dot(
                    w, vg, preferred_element_type=jnp.float32
                )
                t = lax.dot_general(
                    ones, w, (((1,), (1,)), ((), ())), preferred_element_type=jnp.float32
                )
                out_ref[i, rows:rows + 8, h * rows:(h + 1) * rows] += t

    key_pos = lax.broadcasted_iota(jnp.int32, (rows, page_len), 1)
    if with_own:
        q_pos = lax.broadcasted_iota(jnp.int32, (rows, page_len), 0)
        add_block(ds.index(0), q_refs[ds.index(0)], kn_ref[...], vn_ref[...], key_pos <= q_pos)

    def slot(s, carry):
        d = meta_ref[0, s]
        lim = meta_ref[1, s]
        for i, dd in enumerate(ds):
            @pl.when((d == dd) & (lim > 0))
            def _():
                add_block(i, q_refs[i], kp_ref[s], vp_ref[s], key_pos < lim)

        return carry

    lax.fori_loop(0, slots, slot, 0)


def attend(ds, meta, qs, kp, vp, kn=None, vn=None):
    with_own = kn is not None
    rows, width = qs[0].shape
    slots, page_len, kv_width = kp.shape
    args = [meta, *qs, kp, vp] + ([kn, vn] if with_own else [])
    blocks = slots + (1 if with_own else 0)
    heads = width // HEAD_SIZE
    flops = blocks * heads * rows * page_len * HEAD_SIZE * 4
    cost = pl.CostEstimate(
        flops=flops,
        transcendentals=blocks * heads * rows * page_len * 2,
        bytes_accessed=sum(int(x.size) * x.dtype.itemsize for x in args)
        + len(ds) * (rows + 8) * width * 4,
    )
    return pl.pallas_call(
        functools.partial(_attend_kernel, tuple(ds), with_own),
        out_shape=jax.ShapeDtypeStruct((len(ds), rows + 8, width), jnp.float32),
        in_specs=[pl.BlockSpec(memory_space=pltpu.SMEM)]
        + [pl.BlockSpec(memory_space=pltpu.VMEM)] * (len(args) - 1),
        out_specs=pl.BlockSpec(memory_space=pltpu.VMEM),
        cost_estimate=cost,
    )(*args)


def on_device(
    queries,
    incoming_keys,
    incoming_values,
    cached_key_pages,
    cached_value_pages,
    page_table,
    lengths,
):
    tensor_size = lax.axis_size("tensor")
    n_tok = queries.shape[0]
    q_width = queries.shape[1] // tensor_size
    kv_width = incoming_keys.shape[1] // tensor_size
    packed = jnp.concatenate(
        [
            queries.reshape(n_tok, tensor_size, q_width),
            incoming_keys.reshape(n_tok, tensor_size, kv_width),
            incoming_values.reshape(n_tok, tensor_size, kv_width),
        ],
        axis=2,
    )
    mixed = lax.all_to_all(packed, "tensor", split_axis=1, concat_axis=0, tiled=True)
    rows = mixed.shape[0]
    mixed = mixed.reshape(rows, q_width + 2 * kv_width)
    q_own = mixed[:, :q_width]
    k_new = mixed[:, q_width:q_width + kv_width]
    v_new = mixed[:, q_width + kv_width:]

    pool_size = lax.axis_size("pool")
    holder = lax.axis_index("pool")
    slots_dev = cached_key_pages.shape[0]
    page_len = cached_key_pages.shape[1]
    owners = (holder - jnp.arange(SPAN, dtype=jnp.int32)) % pool_size
    table_rows = jnp.take(page_table, owners, axis=0)
    global_slot = holder * slots_dev + jnp.arange(slots_dev, dtype=jnp.int32)
    matches = table_rows[:, :, None] == global_slot[None, None, :]
    owner_hot = jnp.any(matches, axis=1)
    page_index = jnp.sum(
        jnp.where(matches, jnp.arange(table_rows.shape[1], dtype=jnp.int32)[None, :, None], 0),
        axis=(0, 1),
    )
    distance = jnp.sum(jnp.where(owner_hot, jnp.arange(SPAN, dtype=jnp.int32)[:, None], 0), axis=0)
    owner_len = jnp.take(lengths, owners)
    slot_len = jnp.sum(jnp.where(owner_hot, owner_len[:, None], 0), axis=0)
    limit = jnp.clip(slot_len - page_index * page_len, 0, page_len)
    meta = jnp.stack([distance, limit]).astype(jnp.int32)

    received = [shifted(q_own, "pool", offset) for offset in range(1, SPAN)]
    part_own = attend([0], meta, [q_own], cached_key_pages, cached_value_pages, k_new, v_new)[0]
    *received, part_own = lax.optimization_barrier((*received, part_own))
    received = [q_own] + received

    def part(offset):
        return attend([offset], meta, [received[offset]], cached_key_pages, cached_value_pages)[0]

    total = part(SPAN - 1)
    for offset in range(SPAN - 2, -1, -1):
        moved = shifted(total, "pool", -1)
        here = part(offset) if offset > 0 else part_own
        moved, here = lax.optimization_barrier((moved, here))
        total = here + moved
    heads = q_width // HEAD_SIZE
    numerator = total[:rows].reshape(rows, heads, HEAD_SIZE)
    totals = total[rows, : heads * rows].reshape(heads, rows)
    attended = numerator / jnp.transpose(totals)[:, :, None]
    attended = attended.reshape(rows, q_width).astype(jnp.bfloat16)
    return lax.all_to_all(attended, "tensor", split_axis=0, concat_axis=1, tiled=True)


def solution(mesh):
    placed = (
        P(("pool", "tensor"), None),
        P(("pool", "tensor"), None),
        P(("pool", "tensor"), None),
        P("pool", None, "tensor"),
        P("pool", None, "tensor"),
        P(),
        P(),
    )
    return jax.shard_map(
        on_device,
        mesh=mesh,
        in_specs=placed,
        out_specs=P(("pool", "tensor"), None),
        check_vma=False,
    )
```

```python
import functools

import jax
import jax.numpy as jnp
from jax import lax
from jax.experimental import pallas as pl
from jax.experimental.pallas import tpu as pltpu
from jax.sharding import PartitionSpec as P

QUERY_HEADS = 16
KEY_VALUE_HEADS = 8
HEAD_SIZE = 256
SPAN = 4

SOFTCAP = 50.0
SCORE_SCALE = HEAD_SIZE ** (-0.5)


def shifted(block, axis, distance):
    devices = range(lax.axis_size(axis))
    route = [((i - distance) % len(devices), i) for i in devices]
    return lax.ppermute(block, axis, route)


def _attend_kernel(dist, with_own, meta_ref, q_ref, kp_hbm, vp_hbm, *refs):
    if with_own:
        kn_ref, vn_ref = refs[0], refs[1]
        refs = refs[2:]
    out_ref, kbuf, vbuf, sem = refs
    rows = q_ref.shape[0]
    page_len, kv_width = kbuf.shape[1], kbuf.shape[2]
    kv_local = kv_width // HEAD_SIZE
    group = QUERY_HEADS // KEY_VALUE_HEADS
    count = meta_ref[dist, 2, 0]

    def copies(i, b):
        s = meta_ref[dist, 0, i]
        return (
            pltpu.make_async_copy(kp_hbm.at[s], kbuf.at[b], sem.at[0, b]),
            pltpu.make_async_copy(vp_hbm.at[s], vbuf.at[b], sem.at[1, b]),
        )

    @pl.when(count > 0)
    def _():
        for c in copies(0, 0):
            c.start()

    out_ref[...] = jnp.zeros(out_ref.shape, jnp.float32)
    ones = jnp.ones((8, page_len), jnp.bfloat16)

    def add_block(k, v, visible):
        for g in range(kv_local):
            kg = k[:, g * HEAD_SIZE:(g + 1) * HEAD_SIZE]
            vg = v[:, g * HEAD_SIZE:(g + 1) * HEAD_SIZE]
            for a in range(group):
                h = g * group + a
                col = h * HEAD_SIZE
                q = q_ref[:, col:col + HEAD_SIZE]
                s = lax.dot_general(
                    q, kg, (((1,), (1,)), ((), ())), preferred_element_type=jnp.float32
                ) * SCORE_SCALE
                w = jnp.where(visible, jnp.exp(SOFTCAP * jnp.tanh(s / SOFTCAP)), 0.0).astype(
                    jnp.bfloat16
                )
                out_ref[:rows, col:col + HEAD_SIZE] += jnp.dot(
                    w, vg, preferred_element_type=jnp.float32
                )
                t = lax.dot_general(
                    ones, w, (((1,), (1,)), ((), ())), preferred_element_type=jnp.float32
                )
                out_ref[rows:rows + 8, h * rows:(h + 1) * rows] += t

    key_pos = lax.broadcasted_iota(jnp.int32, (rows, page_len), 1)
    if with_own:
        q_pos = lax.broadcasted_iota(jnp.int32, (rows, page_len), 0)
        add_block(kn_ref[...], vn_ref[...], key_pos <= q_pos)

    def slot(i, carry):
        b = i % 2

        @pl.when(i + 1 < count)
        def _():
            for c in copies(i + 1, 1 - b):
                c.start()

        for c in copies(i, b):
            c.wait()
        add_block(kbuf[b], vbuf[b], key_pos < meta_ref[dist, 1, i])
        return carry

    lax.fori_loop(0, count, slot, 0)


def attend(dist, meta, q, kp, vp, kn=None, vn=None):
    with_own = kn is not None
    rows, width = q.shape
    slots, page_len, kv_width = kp.shape
    args = [meta, q, kp, vp] + ([kn, vn] if with_own else [])
    blocks = slots // SPAN + (1 if with_own else 0)
    heads = width // HEAD_SIZE
    cost = pl.CostEstimate(
        flops=blocks * heads * rows * page_len * HEAD_SIZE * 4,
        transcendentals=blocks * heads * rows * page_len * 2,
        bytes_accessed=int(q.size) * 2 + blocks * page_len * kv_width * 4
        + (rows + 8) * width * 4,
    )
    vmem = pl.BlockSpec(memory_space=pltpu.VMEM)
    hbm = pl.BlockSpec(memory_space=pl.ANY)
    return pl.pallas_call(
        functools.partial(_attend_kernel, dist, with_own),
        out_shape=jax.ShapeDtypeStruct((rows + 8, width), jnp.float32),
        in_specs=[pl.BlockSpec(memory_space=pltpu.SMEM), vmem, hbm, hbm]
        + [vmem] * (2 if with_own else 0),
        out_specs=vmem,
        scratch_shapes=[
            pltpu.VMEM((2, page_len, kv_width), kp.dtype),
            pltpu.VMEM((2, page_len, kv_width), vp.dtype),
            pltpu.SemaphoreType.DMA((2, 2)),
        ],
        cost_estimate=cost,
    )(*args)


def on_device(
    queries,
    incoming_keys,
    incoming_values,
    cached_key_pages,
    cached_value_pages,
    page_table,
    lengths,
):
    tensor_size = lax.axis_size("tensor")
    n_tok = queries.shape[0]
    q_width = queries.shape[1] // tensor_size
    kv_width = incoming_keys.shape[1] // tensor_size
    packed = jnp.concatenate(
        [
            queries.reshape(n_tok, tensor_size, q_width),
            incoming_keys.reshape(n_tok, tensor_size, kv_width),
            incoming_values.reshape(n_tok, tensor_size, kv_width),
        ],
        axis=2,
    )
    mixed = lax.all_to_all(packed, "tensor", split_axis=1, concat_axis=0, tiled=True)
    rows = mixed.shape[0]
    mixed = mixed.reshape(rows, q_width + 2 * kv_width)
    q_own = mixed[:, :q_width]
    k_new = mixed[:, q_width:q_width + kv_width]
    v_new = mixed[:, q_width + kv_width:]

    pool_size = lax.axis_size("pool")
    holder = lax.axis_index("pool")
    slots_dev = cached_key_pages.shape[0]
    page_len = cached_key_pages.shape[1]
    owners = (holder - jnp.arange(SPAN, dtype=jnp.int32)) % pool_size
    table_rows = jnp.take(page_table, owners, axis=0)
    global_slot = holder * slots_dev + jnp.arange(slots_dev, dtype=jnp.int32)
    matches = table_rows[:, :, None] == global_slot[None, None, :]
    owner_hot = jnp.any(matches, axis=1)
    page_index = jnp.sum(
        jnp.where(matches, jnp.arange(table_rows.shape[1], dtype=jnp.int32)[None, :, None], 0),
        axis=(0, 1),
    )
    distance = jnp.sum(jnp.where(owner_hot, jnp.arange(SPAN, dtype=jnp.int32)[:, None], 0), axis=0)
    owner_len = jnp.take(lengths, owners)
    slot_len = jnp.sum(jnp.where(owner_hot, owner_len[:, None], 0), axis=0)
    limit = jnp.clip(slot_len - page_index * page_len, 0, page_len)
    wanted = (distance[None, :] == jnp.arange(SPAN, dtype=jnp.int32)[:, None]) & (limit > 0)
    rank = jnp.cumsum(wanted.astype(jnp.int32), axis=1) - 1
    place = wanted[:, :, None] & (rank[:, :, None] == jnp.arange(slots_dev, dtype=jnp.int32))
    order = jnp.sum(jnp.where(place, jnp.arange(slots_dev, dtype=jnp.int32)[None, :, None], 0), axis=1)
    order_limit = jnp.sum(jnp.where(place, limit[None, :, None], 0), axis=1)
    count = jnp.broadcast_to(jnp.sum(wanted.astype(jnp.int32), axis=1, keepdims=True), (SPAN, slots_dev))
    meta = jnp.stack([order, order_limit, count], axis=1).astype(jnp.int32)

    received = [shifted(q_own, "pool", offset) for offset in range(1, SPAN)]
    part_own = attend(0, meta, q_own, cached_key_pages, cached_value_pages, k_new, v_new)
    *received, part_own = lax.optimization_barrier((*received, part_own))
    received = [q_own] + received

    def part(offset):
        return attend(offset, meta, received[offset], cached_key_pages, cached_value_pages)

    total = part(SPAN - 1)
    for offset in range(SPAN - 2, -1, -1):
        moved = shifted(total, "pool", -1)
        here = part(offset) if offset > 0 else part_own
        moved, here = lax.optimization_barrier((moved, here))
        total = here + moved
    heads = q_width // HEAD_SIZE
    numerator = total[:rows].reshape(rows, heads, HEAD_SIZE)
    totals = total[rows, : heads * rows].reshape(heads, rows)
    attended = numerator / jnp.transpose(totals)[:, :, None]
    attended = attended.reshape(rows, q_width).astype(jnp.bfloat16)
    return lax.all_to_all(attended, "tensor", split_axis=0, concat_axis=1, tiled=True)


def solution(mesh):
    placed = (
        P(("pool", "tensor"), None),
        P(("pool", "tensor"), None),
        P(("pool", "tensor"), None),
        P("pool", None, "tensor"),
        P("pool", None, "tensor"),
        P(),
        P(),
    )
    return jax.shard_map(
        on_device,
        mesh=mesh,
        in_specs=placed,
        out_specs=P(("pool", "tensor"), None),
        check_vma=False,
    )
```

```python
import functools

import jax
import jax.numpy as jnp
from jax import lax
from jax.experimental import pallas as pl
from jax.experimental.pallas import tpu as pltpu
from jax.sharding import PartitionSpec as P

QUERY_HEADS = 16
KEY_VALUE_HEADS = 8
HEAD_SIZE = 256
SPAN = 4

SOFTCAP = 50.0
SCORE_SCALE = HEAD_SIZE ** (-0.5)


def shifted(block, axis, distance):
    devices = range(lax.axis_size(axis))
    route = [((i - distance) % len(devices), i) for i in devices]
    return lax.ppermute(block, axis, route)


def _attend_kernel(dist, with_own, meta_ref, q_ref, kp_hbm, vp_hbm, *refs):
    if with_own:
        kn_ref, vn_ref = refs[0], refs[1]
        refs = refs[2:]
    out_ref, kbuf, vbuf, sem = refs
    rows = q_ref.shape[0]
    page_len, kv_width = kbuf.shape[1], kbuf.shape[2]
    kv_local = kv_width // HEAD_SIZE
    group = QUERY_HEADS // KEY_VALUE_HEADS
    count = meta_ref[dist, 2, 0]

    def copies(i):
        s = meta_ref[dist, 0, i]
        return (
            pltpu.make_async_copy(kp_hbm.at[s], kbuf.at[i], sem.at[0, i]),
            pltpu.make_async_copy(vp_hbm.at[s], vbuf.at[i], sem.at[1, i]),
        )

    def request(i, carry):
        for c in copies(i):
            c.start()
        return carry

    lax.fori_loop(0, count, request, 0)

    out_ref[...] = jnp.zeros(out_ref.shape, jnp.float32)
    ones = jnp.ones((8, page_len), jnp.bfloat16)

    stacked = [
        jnp.concatenate(
            [q_ref[:, (g * group + a) * HEAD_SIZE:(g * group + a + 1) * HEAD_SIZE] for a in range(group)],
            axis=0,
        )
        for g in range(kv_local)
    ]

    def add_block(k, v, visible):
        for g in range(kv_local):
            kg = k[:, g * HEAD_SIZE:(g + 1) * HEAD_SIZE]
            vg = v[:, g * HEAD_SIZE:(g + 1) * HEAD_SIZE]
            s = lax.dot_general(
                stacked[g], kg, (((1,), (1,)), ((), ())), preferred_element_type=jnp.float32
            ) * SCORE_SCALE
            w = jnp.where(visible, jnp.exp(SOFTCAP * jnp.tanh(s / SOFTCAP)), 0.0).astype(
                jnp.bfloat16
            )
            pv = jnp.dot(w, vg, preferred_element_type=jnp.float32)
            t = lax.dot_general(
                ones, w, (((1,), (1,)), ((), ())), preferred_element_type=jnp.float32
            )
            for a in range(group):
                h = g * group + a
                col = h * HEAD_SIZE
                out_ref[:rows, col:col + HEAD_SIZE] += pv[a * rows:(a + 1) * rows]
            out_ref[rows:rows + 8, g * group * rows:(g + 1) * group * rows] += t

    key_pos = lax.broadcasted_iota(jnp.int32, (group * rows, page_len), 1)
    if with_own:
        q_pos = lax.broadcasted_iota(jnp.int32, (group * rows, page_len), 0) % rows
        add_block(kn_ref[...], vn_ref[...], key_pos <= q_pos)

    def slot(i, carry):
        for c in copies(i):
            c.wait()
        add_block(kbuf[i], vbuf[i], key_pos < meta_ref[dist, 1, i])
        return carry

    lax.fori_loop(0, count, slot, 0)


def attend(dist, meta, q, kp, vp, kn=None, vn=None):
    with_own = kn is not None
    rows, width = q.shape
    slots, page_len, kv_width = kp.shape
    args = [meta, q, kp, vp] + ([kn, vn] if with_own else [])
    blocks = slots // SPAN + (1 if with_own else 0)
    heads = width // HEAD_SIZE
    cost = pl.CostEstimate(
        flops=blocks * heads * rows * page_len * HEAD_SIZE * 4,
        transcendentals=blocks * heads * rows * page_len * 2,
        bytes_accessed=int(q.size) * 2 + blocks * page_len * kv_width * 4
        + (rows + 8) * width * 4,
    )
    vmem = pl.BlockSpec(memory_space=pltpu.VMEM)
    hbm = pl.BlockSpec(memory_space=pl.ANY)
    return pl.pallas_call(
        functools.partial(_attend_kernel, dist, with_own),
        out_shape=jax.ShapeDtypeStruct((rows + 8, width), jnp.float32),
        in_specs=[pl.BlockSpec(memory_space=pltpu.SMEM), vmem, hbm, hbm]
        + [vmem] * (2 if with_own else 0),
        out_specs=vmem,
        scratch_shapes=[
            pltpu.VMEM((slots, page_len, kv_width), kp.dtype),
            pltpu.VMEM((slots, page_len, kv_width), vp.dtype),
            pltpu.SemaphoreType.DMA((2, slots)),
        ],
        cost_estimate=cost,
    )(*args)


def on_device(
    queries,
    incoming_keys,
    incoming_values,
    cached_key_pages,
    cached_value_pages,
    page_table,
    lengths,
):
    tensor_size = lax.axis_size("tensor")
    n_tok = queries.shape[0]
    q_width = queries.shape[1] // tensor_size
    kv_width = incoming_keys.shape[1] // tensor_size
    packed = jnp.concatenate(
        [
            queries.reshape(n_tok, tensor_size, q_width),
            incoming_keys.reshape(n_tok, tensor_size, kv_width),
            incoming_values.reshape(n_tok, tensor_size, kv_width),
        ],
        axis=2,
    )
    mixed = lax.all_to_all(packed, "tensor", split_axis=1, concat_axis=0, tiled=True)
    rows = mixed.shape[0]
    mixed = mixed.reshape(rows, q_width + 2 * kv_width)
    q_own = mixed[:, :q_width]
    k_new = mixed[:, q_width:q_width + kv_width]
    v_new = mixed[:, q_width + kv_width:]

    pool_size = lax.axis_size("pool")
    holder = lax.axis_index("pool")
    slots_dev = cached_key_pages.shape[0]
    page_len = cached_key_pages.shape[1]
    owners = (holder - jnp.arange(SPAN, dtype=jnp.int32)) % pool_size
    table_rows = jnp.take(page_table, owners, axis=0)
    global_slot = holder * slots_dev + jnp.arange(slots_dev, dtype=jnp.int32)
    matches = table_rows[:, :, None] == global_slot[None, None, :]
    owner_hot = jnp.any(matches, axis=1)
    page_index = jnp.sum(
        jnp.where(matches, jnp.arange(table_rows.shape[1], dtype=jnp.int32)[None, :, None], 0),
        axis=(0, 1),
    )
    distance = jnp.sum(jnp.where(owner_hot, jnp.arange(SPAN, dtype=jnp.int32)[:, None], 0), axis=0)
    owner_len = jnp.take(lengths, owners)
    slot_len = jnp.sum(jnp.where(owner_hot, owner_len[:, None], 0), axis=0)
    limit = jnp.clip(slot_len - page_index * page_len, 0, page_len)
    wanted = (distance[None, :] == jnp.arange(SPAN, dtype=jnp.int32)[:, None]) & (limit > 0)
    rank = jnp.cumsum(wanted.astype(jnp.int32), axis=1) - 1
    place = wanted[:, :, None] & (rank[:, :, None] == jnp.arange(slots_dev, dtype=jnp.int32))
    order = jnp.sum(jnp.where(place, jnp.arange(slots_dev, dtype=jnp.int32)[None, :, None], 0), axis=1)
    order_limit = jnp.sum(jnp.where(place, limit[None, :, None], 0), axis=1)
    count = jnp.broadcast_to(jnp.sum(wanted.astype(jnp.int32), axis=1, keepdims=True), (SPAN, slots_dev))
    meta = jnp.stack([order, order_limit, count], axis=1).astype(jnp.int32)

    received = [shifted(q_own, "pool", offset) for offset in range(1, SPAN)]
    part_own = attend(0, meta, q_own, cached_key_pages, cached_value_pages, k_new, v_new)
    *received, part_own = lax.optimization_barrier((*received, part_own))
    received = [q_own] + received

    def part(offset):
        return attend(offset, meta, received[offset], cached_key_pages, cached_value_pages)

    total = part(SPAN - 1)
    for offset in range(SPAN - 2, -1, -1):
        moved = shifted(total, "pool", -1)
        here = part(offset) if offset > 0 else part_own
        moved, here = lax.optimization_barrier((moved, here))
        total = here + moved
    heads = q_width // HEAD_SIZE
    numerator = total[:rows].reshape(rows, heads, HEAD_SIZE)
    totals = total[rows, : heads * rows].reshape(heads, rows)
    attended = numerator / jnp.transpose(totals)[:, :, None]
    attended = attended.reshape(rows, q_width).astype(jnp.bfloat16)
    return lax.all_to_all(attended, "tensor", split_axis=0, concat_axis=1, tiled=True)


def solution(mesh):
    placed = (
        P(("pool", "tensor"), None),
        P(("pool", "tensor"), None),
        P(("pool", "tensor"), None),
        P("pool", None, "tensor"),
        P("pool", None, "tensor"),
        P(),
        P(),
    )
    return jax.shard_map(
        on_device,
        mesh=mesh,
        in_specs=placed,
        out_specs=P(("pool", "tensor"), None),
        check_vma=False,
    )
```

```python
import functools

import jax
import jax.numpy as jnp
from jax import lax
from jax.experimental import pallas as pl
from jax.experimental.pallas import tpu as pltpu
from jax.sharding import PartitionSpec as P

QUERY_HEADS = 16
KEY_VALUE_HEADS = 8
HEAD_SIZE = 256
SPAN = 4

SOFTCAP = 50.0
SCORE_SCALE = HEAD_SIZE ** (-0.5)


def shifted(block, axis, distance):
    devices = range(lax.axis_size(axis))
    route = [((i - distance) % len(devices), i) for i in devices]
    return lax.ppermute(block, axis, route)


def _attend_kernel(group_index, n_dist, with_own, meta_ref, *refs):
    q_refs = refs[:n_dist]
    kp_hbm, vp_hbm = refs[n_dist], refs[n_dist + 1]
    refs = refs[n_dist + 2:]
    if with_own:
        kn_ref, vn_ref = refs[0], refs[1]
        refs = refs[2:]
    out_ref, stacked, kbuf, vbuf, sem = refs
    rows = q_refs[0].shape[0]
    page_len, kv_width = kbuf.shape[1], kbuf.shape[2]
    kv_local = kv_width // HEAD_SIZE
    group = QUERY_HEADS // KEY_VALUE_HEADS
    count = meta_ref[group_index, 3, 0]

    def copies(i):
        s = meta_ref[group_index, 0, i]
        return (
            pltpu.make_async_copy(kp_hbm.at[s], kbuf.at[i], sem.at[0, i]),
            pltpu.make_async_copy(vp_hbm.at[s], vbuf.at[i], sem.at[1, i]),
        )

    def request(i, carry):
        for c in copies(i):
            c.start()
        return carry

    lax.fori_loop(0, count, request, 0)

    for j in range(n_dist):
        for g in range(kv_local):
            for a in range(group):
                col = (g * group + a) * HEAD_SIZE
                stacked[j, g, a * rows:(a + 1) * rows, :] = q_refs[j][:, col:col + HEAD_SIZE]
    out_ref[...] = jnp.zeros(out_ref.shape, jnp.float32)
    ones = jnp.ones((8, page_len), jnp.bfloat16)

    def add_block(j, k, v, visible):
        for g in range(kv_local):
            kg = k[:, g * HEAD_SIZE:(g + 1) * HEAD_SIZE]
            vg = v[:, g * HEAD_SIZE:(g + 1) * HEAD_SIZE]
            s = lax.dot_general(
                stacked[j, g], kg, (((1,), (1,)), ((), ())), preferred_element_type=jnp.float32
            ) * SCORE_SCALE
            w = jnp.where(visible, jnp.exp(SOFTCAP * jnp.tanh(s / SOFTCAP)), 0.0).astype(
                jnp.bfloat16
            )
            pv = jnp.dot(w, vg, preferred_element_type=jnp.float32)
            t = lax.dot_general(
                ones, w, (((1,), (1,)), ((), ())), preferred_element_type=jnp.float32
            )
            for a in range(group):
                col = (g * group + a) * HEAD_SIZE
                out_ref[j, :rows, col:col + HEAD_SIZE] += pv[a * rows:(a + 1) * rows]
            out_ref[j, rows:rows + 8, g * group * rows:(g + 1) * group * rows] += t

    key_pos = lax.broadcasted_iota(jnp.int32, (group * rows, page_len), 1)
    if with_own:
        q_pos = lax.broadcasted_iota(jnp.int32, (group * rows, page_len), 0) % rows
        add_block(0, kn_ref[...], vn_ref[...], key_pos <= q_pos)

    def slot(i, carry):
        for c in copies(i):
            c.wait()
        add_block(
            meta_ref[group_index, 2, i], kbuf[i], vbuf[i], key_pos < meta_ref[group_index, 1, i]
        )
        return carry

    lax.fori_loop(0, count, slot, 0)


def attend(group_index, meta, qs, kp, vp, kn=None, vn=None):
    with_own = kn is not None
    n_dist = len(qs)
    rows, width = qs[0].shape
    slots, page_len, kv_width = kp.shape
    args = [meta, *qs, kp, vp] + ([kn, vn] if with_own else [])
    blocks = n_dist * slots // SPAN + (1 if with_own else 0)
    heads = width // HEAD_SIZE
    cost = pl.CostEstimate(
        flops=blocks * heads * rows * page_len * HEAD_SIZE * 4,
        transcendentals=blocks * heads * rows * page_len * 2,
        bytes_accessed=n_dist * int(qs[0].size) * 2 + blocks * page_len * kv_width * 4
        + n_dist * (rows + 8) * width * 4,
    )
    vmem = pl.BlockSpec(memory_space=pltpu.VMEM)
    hbm = pl.BlockSpec(memory_space=pl.ANY)
    group = QUERY_HEADS // KEY_VALUE_HEADS
    kv_local = kv_width // HEAD_SIZE
    return pl.pallas_call(
        functools.partial(_attend_kernel, group_index, n_dist, with_own),
        out_shape=jax.ShapeDtypeStruct((n_dist, rows + 8, width), jnp.float32),
        in_specs=[pl.BlockSpec(memory_space=pltpu.SMEM)] + [vmem] * n_dist + [hbm, hbm]
        + [vmem] * (2 if with_own else 0),
        out_specs=vmem,
        scratch_shapes=[
            pltpu.VMEM((n_dist, kv_local, group * rows, HEAD_SIZE), qs[0].dtype),
            pltpu.VMEM((slots, page_len, kv_width), kp.dtype),
            pltpu.VMEM((slots, page_len, kv_width), vp.dtype),
            pltpu.SemaphoreType.DMA((2, slots)),
        ],
        cost_estimate=cost,
    )(*args)


def on_device(
    queries,
    incoming_keys,
    incoming_values,
    cached_key_pages,
    cached_value_pages,
    page_table,
    lengths,
):
    tensor_size = lax.axis_size("tensor")
    n_tok = queries.shape[0]
    q_width = queries.shape[1] // tensor_size
    kv_width = incoming_keys.shape[1] // tensor_size
    packed = jnp.concatenate(
        [
            queries.reshape(n_tok, tensor_size, q_width),
            incoming_keys.reshape(n_tok, tensor_size, kv_width),
            incoming_values.reshape(n_tok, tensor_size, kv_width),
        ],
        axis=2,
    )
    mixed = lax.all_to_all(packed, "tensor", split_axis=1, concat_axis=0, tiled=True)
    rows = mixed.shape[0]
    mixed = mixed.reshape(rows, q_width + 2 * kv_width)
    q_own = mixed[:, :q_width]
    k_new = mixed[:, q_width:q_width + kv_width]
    v_new = mixed[:, q_width + kv_width:]

    pool_size = lax.axis_size("pool")
    holder = lax.axis_index("pool")
    slots_dev = cached_key_pages.shape[0]
    page_len = cached_key_pages.shape[1]
    owners = (holder - jnp.arange(SPAN, dtype=jnp.int32)) % pool_size
    table_rows = jnp.take(page_table, owners, axis=0)
    global_slot = holder * slots_dev + jnp.arange(slots_dev, dtype=jnp.int32)
    matches = table_rows[:, :, None] == global_slot[None, None, :]
    owner_hot = jnp.any(matches, axis=1)
    page_index = jnp.sum(
        jnp.where(matches, jnp.arange(table_rows.shape[1], dtype=jnp.int32)[None, :, None], 0),
        axis=(0, 1),
    )
    distance = jnp.sum(jnp.where(owner_hot, jnp.arange(SPAN, dtype=jnp.int32)[:, None], 0), axis=0)
    owner_len = jnp.take(lengths, owners)
    slot_len = jnp.sum(jnp.where(owner_hot, owner_len[:, None], 0), axis=0)
    limit = jnp.clip(slot_len - page_index * page_len, 0, page_len)
    groups = [(0,), tuple(range(1, SPAN))]
    slot_ids = jnp.arange(slots_dev, dtype=jnp.int32)
    rows_of = []
    for dists in groups:
        wanted = (distance >= dists[0]) & (distance <= dists[-1]) & (limit > 0)
        rank = jnp.cumsum(wanted.astype(jnp.int32)) - 1
        place = wanted[:, None] & (rank[:, None] == slot_ids[None, :])
        pick = lambda values: jnp.sum(jnp.where(place, values[:, None], 0), axis=0)
        rows_of.append(jnp.stack([
            pick(slot_ids),
            pick(limit),
            pick(distance - dists[0]),
            jnp.broadcast_to(jnp.sum(wanted.astype(jnp.int32)), (slots_dev,)),
        ]))
    meta = jnp.stack(rows_of).astype(jnp.int32)

    received = [shifted(q_own, "pool", offset) for offset in range(1, SPAN)]
    part_own = attend(0, meta, [q_own], cached_key_pages, cached_value_pages, k_new, v_new)[0]
    *received, part_own = lax.optimization_barrier((*received, part_own))
    parts = [part_own] + list(attend(1, meta, received, cached_key_pages, cached_value_pages))

    total = parts[SPAN - 1]
    for offset in range(SPAN - 2, -1, -1):
        total = parts[offset] + shifted(total, "pool", -1)
    heads = q_width // HEAD_SIZE
    numerator = total[:rows].reshape(rows, heads, HEAD_SIZE)
    totals = total[rows, : heads * rows].reshape(heads, rows)
    attended = numerator / jnp.transpose(totals)[:, :, None]
    attended = attended.reshape(rows, q_width).astype(jnp.bfloat16)
    return lax.all_to_all(attended, "tensor", split_axis=0, concat_axis=1, tiled=True)


def solution(mesh):
    placed = (
        P(("pool", "tensor"), None),
        P(("pool", "tensor"), None),
        P(("pool", "tensor"), None),
        P("pool", None, "tensor"),
        P("pool", None, "tensor"),
        P(),
        P(),
    )
    return jax.shard_map(
        on_device,
        mesh=mesh,
        in_specs=placed,
        out_specs=P(("pool", "tensor"), None),
        check_vma=False,
    )
```

```python
import functools

import jax
import jax.numpy as jnp
from jax import lax
from jax.experimental import pallas as pl
from jax.experimental.pallas import tpu as pltpu
from jax.sharding import PartitionSpec as P

QUERY_HEADS = 16
KEY_VALUE_HEADS = 8
HEAD_SIZE = 256
SPAN = 4

SOFTCAP = 50.0
SCORE_SCALE = HEAD_SIZE ** (-0.5)


def shifted(block, axis, distance):
    devices = range(lax.axis_size(axis))
    route = [((i - distance) % len(devices), i) for i in devices]
    return lax.ppermute(block, axis, route)


def _attend_kernel(dist, with_own, meta_ref, q_ref, kp_hbm, vp_hbm, *refs):
    if with_own:
        kn_ref, vn_ref = refs[0], refs[1]
        refs = refs[2:]
    out_ref, kbuf, vbuf, sem = refs
    rows = q_ref.shape[0]
    page_len, kv_width = kbuf.shape[1], kbuf.shape[2]
    kv_local = kv_width // HEAD_SIZE
    group = QUERY_HEADS // KEY_VALUE_HEADS
    count = meta_ref[dist, 2, 0]

    def copies(i):
        s = meta_ref[dist, 0, i]
        return (
            pltpu.make_async_copy(kp_hbm.at[s], kbuf.at[i], sem.at[0, i]),
            pltpu.make_async_copy(vp_hbm.at[s], vbuf.at[i], sem.at[1, i]),
        )

    def request(i, carry):
        for c in copies(i):
            c.start()
        return carry

    lax.fori_loop(0, count, request, 0)

    out_ref[...] = jnp.zeros(out_ref.shape, jnp.float32)
    ones = jnp.ones((8, page_len), jnp.bfloat16)

    stacked = [
        jnp.concatenate(
            [q_ref[:, (g * group + a) * HEAD_SIZE:(g * group + a + 1) * HEAD_SIZE] for a in range(group)],
            axis=0,
        )
        for g in range(kv_local)
    ]

    def add_block(k, v, visible):
        for g in range(kv_local):
            kg = k[:, g * HEAD_SIZE:(g + 1) * HEAD_SIZE]
            vg = v[:, g * HEAD_SIZE:(g + 1) * HEAD_SIZE]
            s = lax.dot_general(
                stacked[g], kg, (((1,), (1,)), ((), ())), preferred_element_type=jnp.float32
            ) * SCORE_SCALE
            w = jnp.where(visible, jnp.exp(SOFTCAP * jnp.tanh(s / SOFTCAP)), 0.0).astype(
                jnp.bfloat16
            )
            pv = jnp.dot(w, vg, preferred_element_type=jnp.float32)
            t = lax.dot_general(
                ones, w, (((1,), (1,)), ((), ())), preferred_element_type=jnp.float32
            )
            for a in range(group):
                h = g * group + a
                col = h * HEAD_SIZE
                out_ref[:rows, col:col + HEAD_SIZE] += pv[a * rows:(a + 1) * rows]
            out_ref[rows:rows + 8, g * group * rows:(g + 1) * group * rows] += t

    key_pos = lax.broadcasted_iota(jnp.int32, (group * rows, page_len), 1)
    if with_own:
        q_pos = lax.broadcasted_iota(jnp.int32, (group * rows, page_len), 0) % rows
        add_block(kn_ref[...], vn_ref[...], key_pos <= q_pos)

    def slot(i, carry):
        for c in copies(i):
            c.wait()
        add_block(kbuf[i], vbuf[i], key_pos < meta_ref[dist, 1, i])
        return carry

    lax.fori_loop(0, count, slot, 0)


def attend(dist, meta, q, kp, vp, kn=None, vn=None):
    with_own = kn is not None
    rows, width = q.shape
    slots, page_len, kv_width = kp.shape
    args = [meta, q, kp, vp] + ([kn, vn] if with_own else [])
    blocks = slots // SPAN + (1 if with_own else 0)
    heads = width // HEAD_SIZE
    cost = pl.CostEstimate(
        flops=blocks * heads * rows * page_len * HEAD_SIZE * 4,
        transcendentals=blocks * heads * rows * page_len * 2,
        bytes_accessed=int(q.size) * 2 + blocks * page_len * kv_width * 4
        + (rows + 8) * width * 4,
    )
    vmem = pl.BlockSpec(memory_space=pltpu.VMEM)
    hbm = pl.BlockSpec(memory_space=pl.ANY)
    return pl.pallas_call(
        functools.partial(_attend_kernel, dist, with_own),
        out_shape=jax.ShapeDtypeStruct((rows + 8, width), jnp.float32),
        in_specs=[pl.BlockSpec(memory_space=pltpu.SMEM), vmem, hbm, hbm]
        + [vmem] * (2 if with_own else 0),
        out_specs=vmem,
        scratch_shapes=[
            pltpu.VMEM((slots, page_len, kv_width), kp.dtype),
            pltpu.VMEM((slots, page_len, kv_width), vp.dtype),
            pltpu.SemaphoreType.DMA((2, slots)),
        ],
        cost_estimate=cost,
    )(*args)


def on_device(
    queries,
    incoming_keys,
    incoming_values,
    cached_key_pages,
    cached_value_pages,
    page_table,
    lengths,
):
    tensor_size = lax.axis_size("tensor")
    n_tok = queries.shape[0]
    q_width = queries.shape[1] // tensor_size
    kv_width = incoming_keys.shape[1] // tensor_size
    packed = jnp.concatenate(
        [
            queries.reshape(n_tok, tensor_size, q_width),
            incoming_keys.reshape(n_tok, tensor_size, kv_width),
            incoming_values.reshape(n_tok, tensor_size, kv_width),
        ],
        axis=2,
    )
    mixed = lax.all_to_all(packed, "tensor", split_axis=1, concat_axis=0, tiled=True)
    rows = mixed.shape[0]
    mixed = mixed.reshape(rows, q_width + 2 * kv_width)
    q_own = mixed[:, :q_width]
    k_new = mixed[:, q_width:q_width + kv_width]
    v_new = mixed[:, q_width + kv_width:]

    pool_size = lax.axis_size("pool")
    holder = lax.axis_index("pool")
    slots_dev = cached_key_pages.shape[0]
    page_len = cached_key_pages.shape[1]
    owners = (holder - jnp.arange(SPAN, dtype=jnp.int32)) % pool_size
    table_rows = jnp.take(page_table, owners, axis=0)
    global_slot = holder * slots_dev + jnp.arange(slots_dev, dtype=jnp.int32)
    matches = table_rows[:, :, None] == global_slot[None, None, :]
    owner_hot = jnp.any(matches, axis=1)
    page_index = jnp.sum(
        jnp.where(matches, jnp.arange(table_rows.shape[1], dtype=jnp.int32)[None, :, None], 0),
        axis=(0, 1),
    )
    distance = jnp.sum(jnp.where(owner_hot, jnp.arange(SPAN, dtype=jnp.int32)[:, None], 0), axis=0)
    owner_len = jnp.take(lengths, owners)
    slot_len = jnp.sum(jnp.where(owner_hot, owner_len[:, None], 0), axis=0)
    limit = jnp.clip(slot_len - page_index * page_len, 0, page_len)
    wanted = (distance[None, :] == jnp.arange(SPAN, dtype=jnp.int32)[:, None]) & (limit > 0)
    rank = jnp.cumsum(wanted.astype(jnp.int32), axis=1) - 1
    place = wanted[:, :, None] & (rank[:, :, None] == jnp.arange(slots_dev, dtype=jnp.int32))
    order = jnp.sum(jnp.where(place, jnp.arange(slots_dev, dtype=jnp.int32)[None, :, None], 0), axis=1)
    order_limit = jnp.sum(jnp.where(place, limit[None, :, None], 0), axis=1)
    count = jnp.broadcast_to(jnp.sum(wanted.astype(jnp.int32), axis=1, keepdims=True), (SPAN, slots_dev))
    meta = jnp.stack([order, order_limit, count], axis=1).astype(jnp.int32)

    received = [shifted(q_own, "pool", offset) for offset in range(1, SPAN)]
    part_own = attend(0, meta, q_own, cached_key_pages, cached_value_pages, k_new, v_new)
    *received, part_own = lax.optimization_barrier((*received, part_own))
    received = [q_own] + received

    def part(offset):
        return attend(offset, meta, received[offset], cached_key_pages, cached_value_pages)

    half = q_width // 2
    totals = [part(SPAN - 1)[:, :half], part(SPAN - 1)[:, half:]]
    for offset in range(SPAN - 2, -1, -1):
        moved = [shifted(piece, "pool", -1) for piece in totals]
        here = part(offset) if offset > 0 else part_own
        *moved, here = lax.optimization_barrier((*moved, here))
        totals = [here[:, :half] + moved[0], here[:, half:] + moved[1]]
    total = jnp.concatenate(totals, axis=1)
    heads = q_width // HEAD_SIZE
    numerator = total[:rows].reshape(rows, heads, HEAD_SIZE)
    totals = total[rows, : heads * rows].reshape(heads, rows)
    attended = numerator / jnp.transpose(totals)[:, :, None]
    attended = attended.reshape(rows, q_width).astype(jnp.bfloat16)
    return lax.all_to_all(attended, "tensor", split_axis=0, concat_axis=1, tiled=True)


def solution(mesh):
    placed = (
        P(("pool", "tensor"), None),
        P(("pool", "tensor"), None),
        P(("pool", "tensor"), None),
        P("pool", None, "tensor"),
        P("pool", None, "tensor"),
        P(),
        P(),
    )
    return jax.shard_map(
        on_device,
        mesh=mesh,
        in_specs=placed,
        out_specs=P(("pool", "tensor"), None),
        check_vma=False,
    )
```

```python
import functools

import jax
import jax.numpy as jnp
from jax import lax
from jax.experimental import pallas as pl
from jax.experimental.pallas import tpu as pltpu
from jax.sharding import PartitionSpec as P

QUERY_HEADS = 16
KEY_VALUE_HEADS = 8
HEAD_SIZE = 256
SPAN = 4

SOFTCAP = 50.0
SCORE_SCALE = HEAD_SIZE ** (-0.5)


def shifted(block, axis, distance):
    devices = range(lax.axis_size(axis))
    route = [((i - distance) % len(devices), i) for i in devices]
    return lax.ppermute(block, axis, route)


def _attend_kernel(dist, with_own, meta_ref, q_ref, kp_hbm, vp_hbm, *refs):
    if with_own:
        kn_ref, vn_ref = refs[0], refs[1]
        refs = refs[2:]
    out_ref, kbuf, vbuf, sem = refs
    rows = q_ref.shape[0]
    page_len, kv_width = kbuf.shape[1], kbuf.shape[2]
    kv_local = kv_width // HEAD_SIZE
    group = QUERY_HEADS // KEY_VALUE_HEADS
    count = meta_ref[dist, 2, 0]

    def copies(i):
        s = meta_ref[dist, 0, i]
        return (
            pltpu.make_async_copy(kp_hbm.at[s], kbuf.at[i], sem.at[0, i]),
            pltpu.make_async_copy(vp_hbm.at[s], vbuf.at[i], sem.at[1, i]),
        )

    def request(i, carry):
        for c in copies(i):
            c.start()
        return carry

    lax.fori_loop(0, count, request, 0)

    out_ref[...] = jnp.zeros(out_ref.shape, jnp.float32)
    ones = jnp.ones((8, page_len), jnp.bfloat16)

    stacked = [
        jnp.concatenate(
            [q_ref[:, (g * group + a) * HEAD_SIZE:(g * group + a + 1) * HEAD_SIZE] for a in range(group)],
            axis=0,
        )
        for g in range(kv_local)
    ]

    def add_block(k, v, visible):
        for g in range(kv_local):
            kg = k[:, g * HEAD_SIZE:(g + 1) * HEAD_SIZE]
            vg = v[:, g * HEAD_SIZE:(g + 1) * HEAD_SIZE]
            s = lax.dot_general(
                stacked[g], kg, (((1,), (1,)), ((), ())), preferred_element_type=jnp.float32
            ) * SCORE_SCALE
            w = jnp.where(visible, jnp.exp(SOFTCAP * jnp.tanh(s / SOFTCAP)), 0.0).astype(
                jnp.bfloat16
            )
            pv = jnp.dot(w, vg, preferred_element_type=jnp.float32)
            t = lax.dot_general(
                ones, w, (((1,), (1,)), ((), ())), preferred_element_type=jnp.float32
            )
            for a in range(group):
                h = g * group + a
                col = h * HEAD_SIZE
                out_ref[:rows, col:col + HEAD_SIZE] += pv[a * rows:(a + 1) * rows]
            out_ref[rows:rows + 8, g * group * rows:(g + 1) * group * rows] += t

    key_pos = lax.broadcasted_iota(jnp.int32, (group * rows, page_len), 1)
    if with_own:
        q_pos = lax.broadcasted_iota(jnp.int32, (group * rows, page_len), 0) % rows
        add_block(kn_ref[...], vn_ref[...], key_pos <= q_pos)

    def slot(i, carry):
        for c in copies(i):
            c.wait()
        add_block(kbuf[i], vbuf[i], key_pos < meta_ref[dist, 1, i])
        return carry

    lax.fori_loop(0, count, slot, 0)


def attend(dist, meta, q, kp, vp, kn=None, vn=None):
    with_own = kn is not None
    rows, width = q.shape
    slots, page_len, kv_width = kp.shape
    args = [meta, q, kp, vp] + ([kn, vn] if with_own else [])
    blocks = slots // SPAN + (1 if with_own else 0)
    heads = width // HEAD_SIZE
    cost = pl.CostEstimate(
        flops=blocks * heads * rows * page_len * HEAD_SIZE * 4,
        transcendentals=blocks * heads * rows * page_len * 2,
        bytes_accessed=int(q.size) * 2 + blocks * page_len * kv_width * 4
        + (rows + 8) * width * 4,
    )
    vmem = pl.BlockSpec(memory_space=pltpu.VMEM)
    hbm = pl.BlockSpec(memory_space=pl.ANY)
    return pl.pallas_call(
        functools.partial(_attend_kernel, dist, with_own),
        out_shape=jax.ShapeDtypeStruct((rows + 8, width), jnp.float32),
        in_specs=[pl.BlockSpec(memory_space=pltpu.SMEM), vmem, hbm, hbm]
        + [vmem] * (2 if with_own else 0),
        out_specs=vmem,
        scratch_shapes=[
            pltpu.VMEM((slots, page_len, kv_width), kp.dtype),
            pltpu.VMEM((slots, page_len, kv_width), vp.dtype),
            pltpu.SemaphoreType.DMA((2, slots)),
        ],
        cost_estimate=cost,
    )(*args)


def on_device(
    queries,
    incoming_keys,
    incoming_values,
    cached_key_pages,
    cached_value_pages,
    page_table,
    lengths,
):
    tensor_size = lax.axis_size("tensor")
    n_tok = queries.shape[0]
    q_width = queries.shape[1] // tensor_size
    kv_width = incoming_keys.shape[1] // tensor_size
    packed = jnp.concatenate(
        [
            queries.reshape(n_tok, tensor_size, q_width),
            incoming_keys.reshape(n_tok, tensor_size, kv_width),
            incoming_values.reshape(n_tok, tensor_size, kv_width),
        ],
        axis=2,
    )
    mixed = lax.all_to_all(packed, "tensor", split_axis=1, concat_axis=0, tiled=True)
    rows = mixed.shape[0]
    mixed = mixed.reshape(rows, q_width + 2 * kv_width)
    q_own = mixed[:, :q_width]
    k_new = mixed[:, q_width:q_width + kv_width]
    v_new = mixed[:, q_width + kv_width:]

    pool_size = lax.axis_size("pool")
    holder = lax.axis_index("pool")
    slots_dev = cached_key_pages.shape[0]
    page_len = cached_key_pages.shape[1]
    owners = (holder - jnp.arange(SPAN, dtype=jnp.int32)) % pool_size
    table_rows = jnp.take(page_table, owners, axis=0)
    global_slot = holder * slots_dev + jnp.arange(slots_dev, dtype=jnp.int32)
    matches = table_rows[:, :, None] == global_slot[None, None, :]
    owner_hot = jnp.any(matches, axis=1)
    page_index = jnp.sum(
        jnp.where(matches, jnp.arange(table_rows.shape[1], dtype=jnp.int32)[None, :, None], 0),
        axis=(0, 1),
    )
    distance = jnp.sum(jnp.where(owner_hot, jnp.arange(SPAN, dtype=jnp.int32)[:, None], 0), axis=0)
    owner_len = jnp.take(lengths, owners)
    slot_len = jnp.sum(jnp.where(owner_hot, owner_len[:, None], 0), axis=0)
    limit = jnp.clip(slot_len - page_index * page_len, 0, page_len)
    wanted = (distance[None, :] == jnp.arange(SPAN, dtype=jnp.int32)[:, None]) & (limit > 0)
    rank = jnp.cumsum(wanted.astype(jnp.int32), axis=1) - 1
    place = wanted[:, :, None] & (rank[:, :, None] == jnp.arange(slots_dev, dtype=jnp.int32))
    order = jnp.sum(jnp.where(place, jnp.arange(slots_dev, dtype=jnp.int32)[None, :, None], 0), axis=1)
    order_limit = jnp.sum(jnp.where(place, limit[None, :, None], 0), axis=1)
    count = jnp.broadcast_to(jnp.sum(wanted.astype(jnp.int32), axis=1, keepdims=True), (SPAN, slots_dev))
    meta = jnp.stack([order, order_limit, count], axis=1).astype(jnp.int32)

    received = [q_own]
    for offset in range(1, SPAN):
        received.append(shifted(received[-1], "pool", 1))
    received = list(lax.optimization_barrier(tuple(received)))

    def part(offset):
        own = (k_new, v_new) if offset == 0 else ()
        return attend(offset, meta, received[offset], cached_key_pages, cached_value_pages, *own)

    total = part(SPAN - 1)
    for offset in range(SPAN - 2, -1, -1):
        moved = shifted(total, "pool", -1)
        moved, here = lax.optimization_barrier((moved, part(offset)))
        total = here + moved
    heads = q_width // HEAD_SIZE
    numerator = total[:rows].reshape(rows, heads, HEAD_SIZE)
    totals = total[rows, : heads * rows].reshape(heads, rows)
    attended = numerator / jnp.transpose(totals)[:, :, None]
    attended = attended.reshape(rows, q_width).astype(jnp.bfloat16)
    return lax.all_to_all(attended, "tensor", split_axis=0, concat_axis=1, tiled=True)


def solution(mesh):
    placed = (
        P(("pool", "tensor"), None),
        P(("pool", "tensor"), None),
        P(("pool", "tensor"), None),
        P("pool", None, "tensor"),
        P("pool", None, "tensor"),
        P(),
        P(),
    )
    return jax.shard_map(
        on_device,
        mesh=mesh,
        in_specs=placed,
        out_specs=P(("pool", "tensor"), None),
        check_vma=False,
    )
```

```python
import functools

import jax
import jax.numpy as jnp
from jax import lax
from jax.experimental import pallas as pl
from jax.experimental.pallas import tpu as pltpu
from jax.sharding import PartitionSpec as P

QUERY_HEADS = 16
KEY_VALUE_HEADS = 8
HEAD_SIZE = 256
SPAN = 4

SOFTCAP = 50.0
SCORE_SCALE = HEAD_SIZE ** (-0.5)


def shifted(block, axis, distance):
    devices = range(lax.axis_size(axis))
    route = [((i - distance) % len(devices), i) for i in devices]
    return lax.ppermute(block, axis, route)


def _attend_kernel(dist, with_own, meta_ref, q_ref, kp_hbm, vp_hbm, *refs):
    if with_own:
        kn_ref, vn_ref = refs[0], refs[1]
        refs = refs[2:]
    out_ref, kbuf, vbuf, sem = refs
    rows = q_ref.shape[0]
    page_len, kv_width = kbuf.shape[1], kbuf.shape[2]
    kv_local = kv_width // HEAD_SIZE
    group = QUERY_HEADS // KEY_VALUE_HEADS
    count = meta_ref[dist, 2, 0]

    def copies(i):
        s = meta_ref[dist, 0, i]
        return (
            pltpu.make_async_copy(kp_hbm.at[s], kbuf.at[i], sem.at[0, i]),
            pltpu.make_async_copy(vp_hbm.at[s], vbuf.at[i], sem.at[1, i]),
        )

    def request(i, carry):
        for c in copies(i):
            c.start()
        return carry

    lax.fori_loop(0, count, request, 0)

    out_ref[...] = jnp.zeros(out_ref.shape, jnp.float32)
    ones = jnp.ones((8, page_len), jnp.bfloat16)

    stacked = [
        jnp.concatenate(
            [q_ref[:, (g * group + a) * HEAD_SIZE:(g * group + a + 1) * HEAD_SIZE] for a in range(group)],
            axis=0,
        )
        for g in range(kv_local)
    ]

    def add_block(k, v, visible):
        for g in range(kv_local):
            kg = k[:, g * HEAD_SIZE:(g + 1) * HEAD_SIZE]
            vg = v[:, g * HEAD_SIZE:(g + 1) * HEAD_SIZE]
            s = lax.dot_general(
                stacked[g], kg, (((1,), (1,)), ((), ())), preferred_element_type=jnp.float32
            ) * SCORE_SCALE
            w = jnp.where(visible, jnp.exp(SOFTCAP * jnp.tanh(s / SOFTCAP)), 0.0).astype(
                jnp.bfloat16
            )
            pv = jnp.dot(w, vg, preferred_element_type=jnp.float32)
            t = lax.dot_general(
                ones, w, (((1,), (1,)), ((), ())), preferred_element_type=jnp.float32
            )
            for a in range(group):
                h = g * group + a
                col = h * HEAD_SIZE
                out_ref[:rows, col:col + HEAD_SIZE] += pv[a * rows:(a + 1) * rows]
            out_ref[rows:rows + 8, g * group * rows:(g + 1) * group * rows] += t

    key_pos = lax.broadcasted_iota(jnp.int32, (group * rows, page_len), 1)
    if with_own:
        q_pos = lax.broadcasted_iota(jnp.int32, (group * rows, page_len), 0) % rows
        add_block(kn_ref[...], vn_ref[...], key_pos <= q_pos)

    def slot(i, carry):
        for c in copies(i):
            c.wait()
        add_block(kbuf[i], vbuf[i], key_pos < meta_ref[dist, 1, i])
        return carry

    lax.fori_loop(0, count, slot, 0)


def attend(dist, meta, q, kp, vp, kn=None, vn=None):
    with_own = kn is not None
    rows, width = q.shape
    slots, page_len, kv_width = kp.shape
    args = [meta, q, kp, vp] + ([kn, vn] if with_own else [])
    blocks = slots // SPAN + (1 if with_own else 0)
    heads = width // HEAD_SIZE
    cost = pl.CostEstimate(
        flops=blocks * heads * rows * page_len * HEAD_SIZE * 4,
        transcendentals=blocks * heads * rows * page_len * 2,
        bytes_accessed=int(q.size) * 2 + blocks * page_len * kv_width * 4
        + (rows + 8) * width * 4,
    )
    vmem = pl.BlockSpec(memory_space=pltpu.VMEM)
    hbm = pl.BlockSpec(memory_space=pl.ANY)
    return pl.pallas_call(
        functools.partial(_attend_kernel, dist, with_own),
        out_shape=jax.ShapeDtypeStruct((rows + 8, width), jnp.float32),
        in_specs=[pl.BlockSpec(memory_space=pltpu.SMEM), vmem, hbm, hbm]
        + [vmem] * (2 if with_own else 0),
        out_specs=vmem,
        scratch_shapes=[
            pltpu.VMEM((slots, page_len, kv_width), kp.dtype),
            pltpu.VMEM((slots, page_len, kv_width), vp.dtype),
            pltpu.SemaphoreType.DMA((2, slots)),
        ],
        cost_estimate=cost,
    )(*args)


def on_device(
    queries,
    incoming_keys,
    incoming_values,
    cached_key_pages,
    cached_value_pages,
    page_table,
    lengths,
):
    tensor_size = lax.axis_size("tensor")
    n_tok = queries.shape[0]
    q_width = queries.shape[1] // tensor_size
    kv_width = incoming_keys.shape[1] // tensor_size
    packed = jnp.concatenate(
        [
            queries.reshape(n_tok, tensor_size, q_width),
            incoming_keys.reshape(n_tok, tensor_size, kv_width),
            incoming_values.reshape(n_tok, tensor_size, kv_width),
        ],
        axis=2,
    )
    mixed = lax.all_to_all(packed, "tensor", split_axis=1, concat_axis=0, tiled=True)
    rows = mixed.shape[0]
    mixed = mixed.reshape(rows, q_width + 2 * kv_width)
    q_own = mixed[:, :q_width]
    k_new = mixed[:, q_width:q_width + kv_width]
    v_new = mixed[:, q_width + kv_width:]

    pool_size = lax.axis_size("pool")
    holder = lax.axis_index("pool")
    slots_dev = cached_key_pages.shape[0]
    page_len = cached_key_pages.shape[1]
    owners = (holder - jnp.arange(SPAN, dtype=jnp.int32)) % pool_size
    table_rows = jnp.take(page_table, owners, axis=0)
    global_slot = holder * slots_dev + jnp.arange(slots_dev, dtype=jnp.int32)
    matches = table_rows[:, :, None] == global_slot[None, None, :]
    owner_hot = jnp.any(matches, axis=1)
    page_index = jnp.sum(
        jnp.where(matches, jnp.arange(table_rows.shape[1], dtype=jnp.int32)[None, :, None], 0),
        axis=(0, 1),
    )
    distance = jnp.sum(jnp.where(owner_hot, jnp.arange(SPAN, dtype=jnp.int32)[:, None], 0), axis=0)
    owner_len = jnp.take(lengths, owners)
    slot_len = jnp.sum(jnp.where(owner_hot, owner_len[:, None], 0), axis=0)
    limit = jnp.clip(slot_len - page_index * page_len, 0, page_len)
    wanted = (distance[None, :] == jnp.arange(SPAN, dtype=jnp.int32)[:, None]) & (limit > 0)
    rank = jnp.cumsum(wanted.astype(jnp.int32), axis=1) - 1
    place = wanted[:, :, None] & (rank[:, :, None] == jnp.arange(slots_dev, dtype=jnp.int32))
    order = jnp.sum(jnp.where(place, jnp.arange(slots_dev, dtype=jnp.int32)[None, :, None], 0), axis=1)
    order_limit = jnp.sum(jnp.where(place, limit[None, :, None], 0), axis=1)
    count = jnp.broadcast_to(jnp.sum(wanted.astype(jnp.int32), axis=1, keepdims=True), (SPAN, slots_dev))
    meta = jnp.stack([order, order_limit, count], axis=1).astype(jnp.int32)

    def part(offset, queries):
        own = (k_new, v_new) if offset == 0 else ()
        return attend(offset, meta, queries, cached_key_pages, cached_value_pages, *own)

    held = q_own
    total = None
    for offset in range(SPAN):
        here = part(offset, held)
        if offset < SPAN - 1:
            nxt = shifted(held, "pool", 1)
            if offset < SPAN - 3:
                nxt, here = lax.optimization_barrier((nxt, here))
        back = here if offset == 0 else shifted(here, "pool", -offset)
        total = back if total is None else total + back
        if offset < SPAN - 1:
            held = nxt
    heads = q_width // HEAD_SIZE
    numerator = total[:rows].reshape(rows, heads, HEAD_SIZE)
    totals = total[rows, : heads * rows].reshape(heads, rows)
    attended = numerator / jnp.transpose(totals)[:, :, None]
    attended = attended.reshape(rows, q_width).astype(jnp.bfloat16)
    return lax.all_to_all(attended, "tensor", split_axis=0, concat_axis=1, tiled=True)


def solution(mesh):
    placed = (
        P(("pool", "tensor"), None),
        P(("pool", "tensor"), None),
        P(("pool", "tensor"), None),
        P("pool", None, "tensor"),
        P("pool", None, "tensor"),
        P(),
        P(),
    )
    return jax.shard_map(
        on_device,
        mesh=mesh,
        in_specs=placed,
        out_specs=P(("pool", "tensor"), None),
        check_vma=False,
    )
```

```python
import functools

import jax
import jax.numpy as jnp
from jax import lax
from jax.experimental import pallas as pl
from jax.experimental.pallas import tpu as pltpu
from jax.sharding import PartitionSpec as P

QUERY_HEADS = 16
KEY_VALUE_HEADS = 8
HEAD_SIZE = 256
SPAN = 4

SOFTCAP = 50.0
SCORE_SCALE = HEAD_SIZE ** (-0.5)


def shifted(block, axis, distance):
    devices = range(lax.axis_size(axis))
    route = [((i - distance) % len(devices), i) for i in devices]
    return lax.ppermute(block, axis, route)


def _attend_kernel(dist, with_own, meta_ref, q_ref, kp_hbm, vp_hbm, *refs):
    if with_own:
        kn_ref, vn_ref = refs[0], refs[1]
        refs = refs[2:]
    out_ref, kbuf, vbuf, sem = refs
    rows = q_ref.shape[0]
    page_len, kv_width = kbuf.shape[1], kbuf.shape[2]
    kv_local = kv_width // HEAD_SIZE
    group = QUERY_HEADS // KEY_VALUE_HEADS
    count = meta_ref[dist, 2, 0]

    def copies(i):
        s = meta_ref[dist, 0, i]
        return (
            pltpu.make_async_copy(kp_hbm.at[s], kbuf.at[i], sem.at[0, i]),
            pltpu.make_async_copy(vp_hbm.at[s], vbuf.at[i], sem.at[1, i]),
        )

    def request(i, carry):
        for c in copies(i):
            c.start()
        return carry

    lax.fori_loop(0, count, request, 0)

    out_ref[...] = jnp.zeros(out_ref.shape, jnp.float32)
    ones = jnp.ones((8, page_len), jnp.bfloat16)

    stacked = [
        jnp.concatenate(
            [q_ref[:, (g * group + a) * HEAD_SIZE:(g * group + a + 1) * HEAD_SIZE] for a in range(group)],
            axis=0,
        )
        for g in range(kv_local)
    ]

    def add_block(k, v, visible):
        for g in range(kv_local):
            kg = k[:, g * HEAD_SIZE:(g + 1) * HEAD_SIZE]
            vg = v[:, g * HEAD_SIZE:(g + 1) * HEAD_SIZE]
            s = lax.dot_general(
                stacked[g], kg, (((1,), (1,)), ((), ())), preferred_element_type=jnp.float32
            ) * SCORE_SCALE
            w = jnp.where(visible, jnp.exp(SOFTCAP * jnp.tanh(s / SOFTCAP)), 0.0).astype(
                jnp.bfloat16
            )
            pv = jnp.dot(w, vg, preferred_element_type=jnp.float32)
            t = lax.dot_general(
                ones, w, (((1,), (1,)), ((), ())), preferred_element_type=jnp.float32
            )
            for a in range(group):
                h = g * group + a
                col = h * HEAD_SIZE
                out_ref[:rows, col:col + HEAD_SIZE] += pv[a * rows:(a + 1) * rows]
            out_ref[rows:rows + 8, g * group * rows:(g + 1) * group * rows] += t

    key_pos = lax.broadcasted_iota(jnp.int32, (group * rows, page_len), 1)
    if with_own:
        q_pos = lax.broadcasted_iota(jnp.int32, (group * rows, page_len), 0) % rows
        add_block(kn_ref[...], vn_ref[...], key_pos <= q_pos)

    def slot(i, carry):
        for c in copies(i):
            c.wait()
        add_block(kbuf[i], vbuf[i], key_pos < meta_ref[dist, 1, i])
        return carry

    lax.fori_loop(0, count, slot, 0)


def attend(dist, meta, q, kp, vp, kn=None, vn=None):
    with_own = kn is not None
    rows, width = q.shape
    slots, page_len, kv_width = kp.shape
    args = [meta, q, kp, vp] + ([kn, vn] if with_own else [])
    blocks = slots // SPAN + (1 if with_own else 0)
    heads = width // HEAD_SIZE
    cost = pl.CostEstimate(
        flops=blocks * heads * rows * page_len * HEAD_SIZE * 4,
        transcendentals=blocks * heads * rows * page_len * 2,
        bytes_accessed=int(q.size) * 2 + blocks * page_len * kv_width * 4
        + (rows + 8) * width * 4,
    )
    vmem = pl.BlockSpec(memory_space=pltpu.VMEM)
    hbm = pl.BlockSpec(memory_space=pl.ANY)
    return pl.pallas_call(
        functools.partial(_attend_kernel, dist, with_own),
        out_shape=jax.ShapeDtypeStruct((rows + 8, width), jnp.float32),
        in_specs=[pl.BlockSpec(memory_space=pltpu.SMEM), vmem, hbm, hbm]
        + [vmem] * (2 if with_own else 0),
        out_specs=vmem,
        scratch_shapes=[
            pltpu.VMEM((slots, page_len, kv_width), kp.dtype),
            pltpu.VMEM((slots, page_len, kv_width), vp.dtype),
            pltpu.SemaphoreType.DMA((2, slots)),
        ],
        cost_estimate=cost,
    )(*args)


def on_device(
    queries,
    incoming_keys,
    incoming_values,
    cached_key_pages,
    cached_value_pages,
    page_table,
    lengths,
):
    tensor_size = lax.axis_size("tensor")
    n_tok = queries.shape[0]
    q_width = queries.shape[1] // tensor_size
    kv_width = incoming_keys.shape[1] // tensor_size
    packed = jnp.concatenate(
        [
            queries.reshape(n_tok, tensor_size, q_width),
            incoming_keys.reshape(n_tok, tensor_size, kv_width),
            incoming_values.reshape(n_tok, tensor_size, kv_width),
        ],
        axis=2,
    )
    mixed = lax.all_to_all(packed, "tensor", split_axis=1, concat_axis=0, tiled=True)
    rows = mixed.shape[0]
    mixed = mixed.reshape(rows, q_width + 2 * kv_width)
    q_own = mixed[:, :q_width]
    k_new = mixed[:, q_width:q_width + kv_width]
    v_new = mixed[:, q_width + kv_width:]

    pool_size = lax.axis_size("pool")
    holder = lax.axis_index("pool")
    slots_dev = cached_key_pages.shape[0]
    page_len = cached_key_pages.shape[1]
    owners = (holder - jnp.arange(SPAN, dtype=jnp.int32)) % pool_size
    table_rows = jnp.take(page_table, owners, axis=0)
    global_slot = holder * slots_dev + jnp.arange(slots_dev, dtype=jnp.int32)
    matches = table_rows[:, :, None] == global_slot[None, None, :]
    owner_hot = jnp.any(matches, axis=1)
    page_index = jnp.sum(
        jnp.where(matches, jnp.arange(table_rows.shape[1], dtype=jnp.int32)[None, :, None], 0),
        axis=(0, 1),
    )
    distance = jnp.sum(jnp.where(owner_hot, jnp.arange(SPAN, dtype=jnp.int32)[:, None], 0), axis=0)
    owner_len = jnp.take(lengths, owners)
    slot_len = jnp.sum(jnp.where(owner_hot, owner_len[:, None], 0), axis=0)
    limit = jnp.clip(slot_len - page_index * page_len, 0, page_len)
    wanted = (distance[None, :] == jnp.arange(SPAN, dtype=jnp.int32)[:, None]) & (limit > 0)
    rank = jnp.cumsum(wanted.astype(jnp.int32), axis=1) - 1
    place = wanted[:, :, None] & (rank[:, :, None] == jnp.arange(slots_dev, dtype=jnp.int32))
    order = jnp.sum(jnp.where(place, jnp.arange(slots_dev, dtype=jnp.int32)[None, :, None], 0), axis=1)
    order_limit = jnp.sum(jnp.where(place, limit[None, :, None], 0), axis=1)
    count = jnp.broadcast_to(jnp.sum(wanted.astype(jnp.int32), axis=1, keepdims=True), (SPAN, slots_dev))
    meta = jnp.stack([order, order_limit, count], axis=1).astype(jnp.int32)

    def part(offset, queries):
        own = (k_new, v_new) if offset == 0 else ()
        return attend(offset, meta, queries, cached_key_pages, cached_value_pages, *own)

    near = shifted(q_own, "pool", 1)
    mid = shifted(q_own, "pool", 2)
    part_own = part(0, q_own)
    near, mid, part_own = lax.optimization_barrier((near, mid, part_own))
    far = shifted(mid, "pool", 1)
    part_near = part(1, near)
    part_mid = part(2, mid)
    far, part_near, part_mid = lax.optimization_barrier((far, part_near, part_mid))
    parts = [part_own, part_near, part_mid, part(3, far)]

    total = parts[SPAN - 1]
    for offset in range(SPAN - 2, -1, -1):
        total = parts[offset] + shifted(total, "pool", -1)
    heads = q_width // HEAD_SIZE
    numerator = total[:rows].reshape(rows, heads, HEAD_SIZE)
    totals = total[rows, : heads * rows].reshape(heads, rows)
    attended = numerator / jnp.transpose(totals)[:, :, None]
    attended = attended.reshape(rows, q_width).astype(jnp.bfloat16)
    return lax.all_to_all(attended, "tensor", split_axis=0, concat_axis=1, tiled=True)


def solution(mesh):
    placed = (
        P(("pool", "tensor"), None),
        P(("pool", "tensor"), None),
        P(("pool", "tensor"), None),
        P("pool", None, "tensor"),
        P("pool", None, "tensor"),
        P(),
        P(),
    )
    return jax.shard_map(
        on_device,
        mesh=mesh,
        in_specs=placed,
        out_specs=P(("pool", "tensor"), None),
        check_vma=False,
    )
```

```python
import functools

import jax
import jax.numpy as jnp
from jax import lax
from jax.experimental import pallas as pl
from jax.experimental.pallas import tpu as pltpu
from jax.sharding import PartitionSpec as P

QUERY_HEADS = 16
KEY_VALUE_HEADS = 8
HEAD_SIZE = 256
SPAN = 4

SOFTCAP = 50.0
SCORE_SCALE = HEAD_SIZE ** (-0.5)


def shifted(block, axis, distance):
    devices = range(lax.axis_size(axis))
    route = [((i - distance) % len(devices), i) for i in devices]
    return lax.ppermute(block, axis, route)


def _attend_kernel(dist, with_own, meta_ref, q_ref, kp_hbm, vp_hbm, *refs):
    if with_own:
        kn_ref, vn_ref = refs[0], refs[1]
        refs = refs[2:]
    out_ref, kbuf, vbuf, sem = refs
    rows = q_ref.shape[0]
    page_len, kv_width = kbuf.shape[1], kbuf.shape[2]
    kv_local = kv_width // HEAD_SIZE
    group = QUERY_HEADS // KEY_VALUE_HEADS
    count = meta_ref[dist, 2, 0]

    def copies(i):
        s = meta_ref[dist, 0, i]
        return (
            pltpu.make_async_copy(kp_hbm.at[s], kbuf.at[i], sem.at[0, i]),
            pltpu.make_async_copy(vp_hbm.at[s], vbuf.at[i], sem.at[1, i]),
        )

    def request(i, carry):
        for c in copies(i):
            c.start()
        return carry

    lax.fori_loop(0, count, request, 0)

    out_ref[...] = jnp.zeros(out_ref.shape, jnp.float32)
    ones = jnp.ones((8, page_len), jnp.bfloat16)

    stacked = [
        jnp.concatenate(
            [q_ref[:, (g * group + a) * HEAD_SIZE:(g * group + a + 1) * HEAD_SIZE] for a in range(group)],
            axis=0,
        )
        for g in range(kv_local)
    ]

    def add_block(k, v, visible):
        for g in range(kv_local):
            kg = k[:, g * HEAD_SIZE:(g + 1) * HEAD_SIZE]
            vg = v[:, g * HEAD_SIZE:(g + 1) * HEAD_SIZE]
            s = lax.dot_general(
                stacked[g], kg, (((1,), (1,)), ((), ())), preferred_element_type=jnp.float32
            ) * SCORE_SCALE
            w = jnp.where(visible, jnp.exp(SOFTCAP * jnp.tanh(s / SOFTCAP)), 0.0).astype(
                jnp.bfloat16
            )
            pv = jnp.dot(w, vg, preferred_element_type=jnp.float32)
            t = lax.dot_general(
                ones, w, (((1,), (1,)), ((), ())), preferred_element_type=jnp.float32
            )
            for a in range(group):
                h = g * group + a
                col = h * HEAD_SIZE
                out_ref[:rows, col:col + HEAD_SIZE] += pv[a * rows:(a + 1) * rows]
            out_ref[rows:rows + 8, g * group * rows:(g + 1) * group * rows] += t

    key_pos = lax.broadcasted_iota(jnp.int32, (group * rows, page_len), 1)
    if with_own:
        q_pos = lax.broadcasted_iota(jnp.int32, (group * rows, page_len), 0) % rows
        add_block(kn_ref[...], vn_ref[...], key_pos <= q_pos)

    def slot(i, carry):
        for c in copies(i):
            c.wait()
        add_block(kbuf[i], vbuf[i], key_pos < meta_ref[dist, 1, i])
        return carry

    lax.fori_loop(0, count, slot, 0)


def attend(dist, meta, q, kp, vp, kn=None, vn=None):
    with_own = kn is not None
    rows, width = q.shape
    slots, page_len, kv_width = kp.shape
    args = [meta, q, kp, vp] + ([kn, vn] if with_own else [])
    blocks = slots // SPAN + (1 if with_own else 0)
    heads = width // HEAD_SIZE
    cost = pl.CostEstimate(
        flops=blocks * heads * rows * page_len * HEAD_SIZE * 4,
        transcendentals=blocks * heads * rows * page_len * 2,
        bytes_accessed=int(q.size) * 2 + blocks * page_len * kv_width * 4
        + (rows + 8) * width * 4,
    )
    vmem = pl.BlockSpec(memory_space=pltpu.VMEM)
    hbm = pl.BlockSpec(memory_space=pl.ANY)
    return pl.pallas_call(
        functools.partial(_attend_kernel, dist, with_own),
        out_shape=jax.ShapeDtypeStruct((rows + 8, width), jnp.float32),
        in_specs=[pl.BlockSpec(memory_space=pltpu.SMEM), vmem, hbm, hbm]
        + [vmem] * (2 if with_own else 0),
        out_specs=vmem,
        scratch_shapes=[
            pltpu.VMEM((slots, page_len, kv_width), kp.dtype),
            pltpu.VMEM((slots, page_len, kv_width), vp.dtype),
            pltpu.SemaphoreType.DMA((2, slots)),
        ],
        cost_estimate=cost,
    )(*args)


def on_device(
    queries,
    incoming_keys,
    incoming_values,
    cached_key_pages,
    cached_value_pages,
    page_table,
    lengths,
):
    tensor_size = lax.axis_size("tensor")
    n_tok = queries.shape[0]
    q_width = queries.shape[1] // tensor_size
    kv_width = incoming_keys.shape[1] // tensor_size
    packed = jnp.concatenate(
        [
            jnp.swapaxes(queries.reshape(n_tok, tensor_size, q_width), 0, 1),
            jnp.swapaxes(incoming_keys.reshape(n_tok, tensor_size, kv_width), 0, 1),
            jnp.swapaxes(incoming_values.reshape(n_tok, tensor_size, kv_width), 0, 1),
        ],
        axis=2,
    )
    mixed = lax.all_to_all(packed, "tensor", split_axis=0, concat_axis=0, tiled=True)
    rows = tensor_size * n_tok
    mixed = mixed.reshape(rows, q_width + 2 * kv_width)
    q_own = mixed[:, :q_width]
    k_new = mixed[:, q_width:q_width + kv_width]
    v_new = mixed[:, q_width + kv_width:]

    pool_size = lax.axis_size("pool")
    holder = lax.axis_index("pool")
    slots_dev = cached_key_pages.shape[0]
    page_len = cached_key_pages.shape[1]
    owners = (holder - jnp.arange(SPAN, dtype=jnp.int32)) % pool_size
    table_rows = jnp.take(page_table, owners, axis=0)
    global_slot = holder * slots_dev + jnp.arange(slots_dev, dtype=jnp.int32)
    matches = table_rows[:, :, None] == global_slot[None, None, :]
    owner_hot = jnp.any(matches, axis=1)
    page_index = jnp.sum(
        jnp.where(matches, jnp.arange(table_rows.shape[1], dtype=jnp.int32)[None, :, None], 0),
        axis=(0, 1),
    )
    distance = jnp.sum(jnp.where(owner_hot, jnp.arange(SPAN, dtype=jnp.int32)[:, None], 0), axis=0)
    owner_len = jnp.take(lengths, owners)
    slot_len = jnp.sum(jnp.where(owner_hot, owner_len[:, None], 0), axis=0)
    limit = jnp.clip(slot_len - page_index * page_len, 0, page_len)
    wanted = (distance[None, :] == jnp.arange(SPAN, dtype=jnp.int32)[:, None]) & (limit > 0)
    rank = jnp.cumsum(wanted.astype(jnp.int32), axis=1) - 1
    place = wanted[:, :, None] & (rank[:, :, None] == jnp.arange(slots_dev, dtype=jnp.int32))
    order = jnp.sum(jnp.where(place, jnp.arange(slots_dev, dtype=jnp.int32)[None, :, None], 0), axis=1)
    order_limit = jnp.sum(jnp.where(place, limit[None, :, None], 0), axis=1)
    count = jnp.broadcast_to(jnp.sum(wanted.astype(jnp.int32), axis=1, keepdims=True), (SPAN, slots_dev))
    meta = jnp.stack([order, order_limit, count], axis=1).astype(jnp.int32)

    received = [shifted(q_own, "pool", offset) for offset in range(1, SPAN)]
    part_own = attend(0, meta, q_own, cached_key_pages, cached_value_pages, k_new, v_new)
    *received, part_own = lax.optimization_barrier((*received, part_own))
    received = [q_own] + received

    def part(offset):
        return attend(offset, meta, received[offset], cached_key_pages, cached_value_pages)

    total = part(SPAN - 1)
    for offset in range(SPAN - 2, -1, -1):
        moved = shifted(total, "pool", -1)
        here = part(offset) if offset > 0 else part_own
        moved, here = lax.optimization_barrier((moved, here))
        total = here + moved
    heads = q_width // HEAD_SIZE
    numerator = total[:rows].reshape(rows, heads, HEAD_SIZE)
    totals = total[rows, : heads * rows].reshape(heads, rows)
    attended = numerator / jnp.transpose(totals)[:, :, None]
    attended = attended.reshape(tensor_size, n_tok, q_width).astype(jnp.bfloat16)
    sent = lax.all_to_all(attended, "tensor", split_axis=0, concat_axis=0, tiled=True)
    return jnp.swapaxes(sent, 0, 1).reshape(n_tok, tensor_size * q_width)


def solution(mesh):
    placed = (
        P(("pool", "tensor"), None),
        P(("pool", "tensor"), None),
        P(("pool", "tensor"), None),
        P("pool", None, "tensor"),
        P("pool", None, "tensor"),
        P(),
        P(),
    )
    return jax.shard_map(
        on_device,
        mesh=mesh,
        in_specs=placed,
        out_specs=P(("pool", "tensor"), None),
        check_vma=False,
    )
```

```python
import functools

import jax
import jax.numpy as jnp
from jax import lax
from jax.experimental import pallas as pl
from jax.experimental.pallas import tpu as pltpu
from jax.sharding import PartitionSpec as P

QUERY_HEADS = 16
KEY_VALUE_HEADS = 8
HEAD_SIZE = 256
SPAN = 4

SOFTCAP = 50.0
SCORE_SCALE = HEAD_SIZE ** (-0.5)


def shifted(block, axis, distance):
    devices = range(lax.axis_size(axis))
    route = [((i - distance) % len(devices), i) for i in devices]
    return lax.ppermute(block, axis, route)


def _attend_kernel(dist, with_own, meta_ref, q_ref, kp_hbm, vp_hbm, *refs):
    if with_own:
        kn_ref, vn_ref = refs[0], refs[1]
        refs = refs[2:]
    out_ref, kbuf, vbuf, sem = refs
    rows = q_ref.shape[0]
    page_len, kv_width = kbuf.shape[1], kbuf.shape[2]
    kv_local = kv_width // HEAD_SIZE
    group = QUERY_HEADS // KEY_VALUE_HEADS
    count = meta_ref[dist, 2, 0]

    def copies(i):
        s = meta_ref[dist, 0, i]
        return (
            pltpu.make_async_copy(kp_hbm.at[s], kbuf.at[i], sem.at[0, i]),
            pltpu.make_async_copy(vp_hbm.at[s], vbuf.at[i], sem.at[1, i]),
        )

    def request(i, carry):
        for c in copies(i):
            c.start()
        return carry

    lax.fori_loop(0, count, request, 0)

    out_ref[...] = jnp.zeros(out_ref.shape, jnp.float32)
    ones = jnp.ones((8, page_len), jnp.bfloat16)

    stacked = [
        jnp.concatenate(
            [q_ref[:, (g * group + a) * HEAD_SIZE:(g * group + a + 1) * HEAD_SIZE] for a in range(group)],
            axis=0,
        )
        for g in range(kv_local)
    ]

    def add_block(k, v, visible):
        for g in range(kv_local):
            kg = k[:, g * HEAD_SIZE:(g + 1) * HEAD_SIZE]
            vg = v[:, g * HEAD_SIZE:(g + 1) * HEAD_SIZE]
            s = lax.dot_general(
                stacked[g], kg, (((1,), (1,)), ((), ())), preferred_element_type=jnp.float32
            ) * SCORE_SCALE
            w = jnp.where(visible, jnp.exp(SOFTCAP * jnp.tanh(s / SOFTCAP)), 0.0).astype(
                jnp.bfloat16
            )
            pv = jnp.dot(w, vg, preferred_element_type=jnp.float32)
            t = lax.dot_general(
                ones, w, (((1,), (1,)), ((), ())), preferred_element_type=jnp.float32
            )
            for a in range(group):
                h = g * group + a
                col = h * HEAD_SIZE
                out_ref[:rows, col:col + HEAD_SIZE] += pv[a * rows:(a + 1) * rows]
            out_ref[rows:rows + 8, g * group * rows:(g + 1) * group * rows] += t

    key_pos = lax.broadcasted_iota(jnp.int32, (group * rows, page_len), 1)
    if with_own:
        q_pos = lax.broadcasted_iota(jnp.int32, (group * rows, page_len), 0) % rows
        add_block(kn_ref[...], vn_ref[...], key_pos <= q_pos)

    def slot(i, carry):
        for c in copies(i):
            c.wait()
        add_block(kbuf[i], vbuf[i], key_pos < meta_ref[dist, 1, i])
        return carry

    lax.fori_loop(0, count, slot, 0)


def attend(dist, meta, q, kp, vp, kn=None, vn=None):
    with_own = kn is not None
    rows, width = q.shape
    slots, page_len, kv_width = kp.shape
    args = [meta, q, kp, vp] + ([kn, vn] if with_own else [])
    blocks = slots // SPAN + (1 if with_own else 0)
    heads = width // HEAD_SIZE
    cost = pl.CostEstimate(
        flops=blocks * heads * rows * page_len * HEAD_SIZE * 4,
        transcendentals=blocks * heads * rows * page_len * 2,
        bytes_accessed=int(q.size) * 2 + blocks * page_len * kv_width * 4
        + (rows + 8) * width * 4,
    )
    vmem = pl.BlockSpec(memory_space=pltpu.VMEM)
    hbm = pl.BlockSpec(memory_space=pl.ANY)
    return pl.pallas_call(
        functools.partial(_attend_kernel, dist, with_own),
        out_shape=jax.ShapeDtypeStruct((rows + 8, width), jnp.float32),
        in_specs=[pl.BlockSpec(memory_space=pltpu.SMEM), vmem, hbm, hbm]
        + [vmem] * (2 if with_own else 0),
        out_specs=vmem,
        scratch_shapes=[
            pltpu.VMEM((slots, page_len, kv_width), kp.dtype),
            pltpu.VMEM((slots, page_len, kv_width), vp.dtype),
            pltpu.SemaphoreType.DMA((2, slots)),
        ],
        cost_estimate=cost,
    )(*args)


def on_device(
    queries,
    incoming_keys,
    incoming_values,
    cached_key_pages,
    cached_value_pages,
    page_table,
    lengths,
):
    tensor_size = lax.axis_size("tensor")
    n_tok = queries.shape[0]
    q_width = queries.shape[1] // tensor_size
    kv_width = incoming_keys.shape[1] // tensor_size
    packed = jnp.concatenate(
        [
            queries.reshape(n_tok, tensor_size, q_width),
            incoming_keys.reshape(n_tok, tensor_size, kv_width),
            incoming_values.reshape(n_tok, tensor_size, kv_width),
        ],
        axis=2,
    )
    mixed = lax.all_to_all(packed, "tensor", split_axis=1, concat_axis=0, tiled=True)
    rows = mixed.shape[0]
    mixed = mixed.reshape(rows, q_width + 2 * kv_width)
    q_own = mixed[:, :q_width]
    k_new = mixed[:, q_width:q_width + kv_width]
    v_new = mixed[:, q_width + kv_width:]

    pool_size = lax.axis_size("pool")
    holder = lax.axis_index("pool")
    slots_dev = cached_key_pages.shape[0]
    page_len = cached_key_pages.shape[1]
    owners = (holder - jnp.arange(SPAN, dtype=jnp.int32)) % pool_size
    table_rows = jnp.take(page_table, owners, axis=0)
    global_slot = holder * slots_dev + jnp.arange(slots_dev, dtype=jnp.int32)
    matches = table_rows[:, :, None] == global_slot[None, None, :]
    owner_hot = jnp.any(matches, axis=1)
    page_index = jnp.sum(
        jnp.where(matches, jnp.arange(table_rows.shape[1], dtype=jnp.int32)[None, :, None], 0),
        axis=(0, 1),
    )
    distance = jnp.sum(jnp.where(owner_hot, jnp.arange(SPAN, dtype=jnp.int32)[:, None], 0), axis=0)
    owner_len = jnp.take(lengths, owners)
    slot_len = jnp.sum(jnp.where(owner_hot, owner_len[:, None], 0), axis=0)
    limit = jnp.clip(slot_len - page_index * page_len, 0, page_len)
    wanted = (distance[None, :] == jnp.arange(SPAN, dtype=jnp.int32)[:, None]) & (limit > 0)
    rank = jnp.cumsum(wanted.astype(jnp.int32), axis=1) - 1
    place = wanted[:, :, None] & (rank[:, :, None] == jnp.arange(slots_dev, dtype=jnp.int32))
    order = jnp.sum(jnp.where(place, jnp.arange(slots_dev, dtype=jnp.int32)[None, :, None], 0), axis=1)
    order_limit = jnp.sum(jnp.where(place, limit[None, :, None], 0), axis=1)
    count = jnp.broadcast_to(jnp.sum(wanted.astype(jnp.int32), axis=1, keepdims=True), (SPAN, slots_dev))
    meta = jnp.stack([order, order_limit, count], axis=1).astype(jnp.int32)

    received = [shifted(q_own, "pool", offset) for offset in range(1, SPAN)]
    part_own = attend(0, meta, q_own, cached_key_pages, cached_value_pages, k_new, v_new)
    *received, part_own = lax.optimization_barrier((*received, part_own))
    received = [q_own] + received

    def part(offset):
        return attend(offset, meta, received[offset], cached_key_pages, cached_value_pages)

    total = part(SPAN - 1)
    for offset in range(SPAN - 2, 0, -1):
        moved = shifted(total, "pool", -1)
        moved, here = lax.optimization_barrier((moved, part(offset)))
        total = here + moved
    total = total + shifted(part_own, "pool", 1)
    heads = q_width // HEAD_SIZE
    numerator = total[:rows].reshape(rows, heads, HEAD_SIZE)
    totals = total[rows, : heads * rows].reshape(heads, rows)
    attended = numerator / jnp.transpose(totals)[:, :, None]
    attended = attended.reshape(rows, q_width).astype(jnp.bfloat16)
    attended = shifted(attended, "pool", -1)
    return lax.all_to_all(attended, "tensor", split_axis=0, concat_axis=1, tiled=True)


def solution(mesh):
    placed = (
        P(("pool", "tensor"), None),
        P(("pool", "tensor"), None),
        P(("pool", "tensor"), None),
        P("pool", None, "tensor"),
        P("pool", None, "tensor"),
        P(),
        P(),
    )
    return jax.shard_map(
        on_device,
        mesh=mesh,
        in_specs=placed,
        out_specs=P(("pool", "tensor"), None),
        check_vma=False,
    )
```

```python
import functools

import jax
import jax.numpy as jnp
from jax import lax
from jax.experimental import pallas as pl
from jax.experimental.pallas import tpu as pltpu
from jax.sharding import PartitionSpec as P

QUERY_HEADS = 16
KEY_VALUE_HEADS = 8
HEAD_SIZE = 256
SPAN = 4

SOFTCAP = 50.0
SCORE_SCALE = HEAD_SIZE ** (-0.5)


def shifted(block, axis, distance):
    devices = range(lax.axis_size(axis))
    route = [((i - distance) % len(devices), i) for i in devices]
    return lax.ppermute(block, axis, route)


def _attend_kernel(dist, with_own, meta_ref, q_ref, kp_hbm, vp_hbm, *refs):
    if with_own:
        kn_ref, vn_ref = refs[0], refs[1]
        refs = refs[2:]
    out_ref, kbuf, vbuf, sem = refs
    rows = q_ref.shape[0]
    page_len, kv_width = kbuf.shape[1], kbuf.shape[2]
    kv_local = kv_width // HEAD_SIZE
    group = QUERY_HEADS // KEY_VALUE_HEADS
    count = meta_ref[dist, 2, 0]

    def copies(i):
        s = meta_ref[dist, 0, i]
        return (
            pltpu.make_async_copy(kp_hbm.at[s], kbuf.at[i], sem.at[0, i]),
            pltpu.make_async_copy(vp_hbm.at[s], vbuf.at[i], sem.at[1, i]),
        )

    def request(i, carry):
        for c in copies(i):
            c.start()
        return carry

    lax.fori_loop(0, count, request, 0)

    out_ref[...] = jnp.zeros(out_ref.shape, jnp.float32)
    ones = jnp.ones((8, page_len), jnp.bfloat16)

    stacked = [
        jnp.concatenate(
            [q_ref[:, (g * group + a) * HEAD_SIZE:(g * group + a + 1) * HEAD_SIZE] for a in range(group)],
            axis=0,
        )
        for g in range(kv_local)
    ]

    def add_block(k, v, visible):
        for g in range(kv_local):
            kg = k[:, g * HEAD_SIZE:(g + 1) * HEAD_SIZE]
            vg = v[:, g * HEAD_SIZE:(g + 1) * HEAD_SIZE]
            s = lax.dot_general(
                stacked[g], kg, (((1,), (1,)), ((), ())), preferred_element_type=jnp.float32
            ) * SCORE_SCALE
            w = jnp.where(visible, jnp.exp(SOFTCAP * jnp.tanh(s / SOFTCAP)), 0.0).astype(
                jnp.bfloat16
            )
            pv = jnp.dot(w, vg, preferred_element_type=jnp.float32)
            t = lax.dot_general(
                ones, w, (((1,), (1,)), ((), ())), preferred_element_type=jnp.float32
            )
            for a in range(group):
                h = g * group + a
                col = h * HEAD_SIZE
                out_ref[:rows, col:col + HEAD_SIZE] += pv[a * rows:(a + 1) * rows]
            out_ref[rows:rows + 8, g * group * rows:(g + 1) * group * rows] += t

    key_pos = lax.broadcasted_iota(jnp.int32, (group * rows, page_len), 1)
    if with_own:
        q_pos = lax.broadcasted_iota(jnp.int32, (group * rows, page_len), 0) % rows
        add_block(kn_ref[...], vn_ref[...], key_pos <= q_pos)

    def slot(i, carry):
        for c in copies(i):
            c.wait()
        add_block(kbuf[i], vbuf[i], key_pos < meta_ref[dist, 1, i])
        return carry

    lax.fori_loop(0, count, slot, 0)


def attend(dist, meta, q, kp, vp, kn=None, vn=None):
    with_own = kn is not None
    rows, width = q.shape
    slots, page_len, kv_width = kp.shape
    args = [meta, q, kp, vp] + ([kn, vn] if with_own else [])
    blocks = slots // SPAN + (1 if with_own else 0)
    heads = width // HEAD_SIZE
    cost = pl.CostEstimate(
        flops=blocks * heads * rows * page_len * HEAD_SIZE * 4,
        transcendentals=blocks * heads * rows * page_len * 2,
        bytes_accessed=int(q.size) * 2 + blocks * page_len * kv_width * 4
        + (rows + 8) * width * 4,
    )
    vmem = pl.BlockSpec(memory_space=pltpu.VMEM)
    hbm = pl.BlockSpec(memory_space=pl.ANY)
    return pl.pallas_call(
        functools.partial(_attend_kernel, dist, with_own),
        out_shape=jax.ShapeDtypeStruct((rows + 8, width), jnp.float32),
        in_specs=[pl.BlockSpec(memory_space=pltpu.SMEM), vmem, hbm, hbm]
        + [vmem] * (2 if with_own else 0),
        out_specs=vmem,
        scratch_shapes=[
            pltpu.VMEM((slots, page_len, kv_width), kp.dtype),
            pltpu.VMEM((slots, page_len, kv_width), vp.dtype),
            pltpu.SemaphoreType.DMA((2, slots)),
        ],
        cost_estimate=cost,
    )(*args)


def on_device(
    queries,
    incoming_keys,
    incoming_values,
    cached_key_pages,
    cached_value_pages,
    page_table,
    lengths,
):
    tensor_size = lax.axis_size("tensor")
    n_tok = queries.shape[0]
    q_width = queries.shape[1] // tensor_size
    kv_width = incoming_keys.shape[1] // tensor_size
    packed = jnp.concatenate(
        [
            queries.reshape(n_tok, tensor_size, q_width),
            incoming_keys.reshape(n_tok, tensor_size, kv_width),
            incoming_values.reshape(n_tok, tensor_size, kv_width),
        ],
        axis=2,
    )
    mixed = lax.all_to_all(packed, "tensor", split_axis=1, concat_axis=0, tiled=True)
    rows = mixed.shape[0]
    mixed = mixed.reshape(rows, q_width + 2 * kv_width)
    q_own = mixed[:, :q_width]
    k_new = mixed[:, q_width:q_width + kv_width]
    v_new = mixed[:, q_width + kv_width:]

    pool_size = lax.axis_size("pool")
    holder = lax.axis_index("pool")
    slots_dev = cached_key_pages.shape[0]
    page_len = cached_key_pages.shape[1]
    owners = (holder - jnp.arange(SPAN, dtype=jnp.int32)) % pool_size
    table_rows = jnp.take(page_table, owners, axis=0)
    global_slot = holder * slots_dev + jnp.arange(slots_dev, dtype=jnp.int32)
    matches = table_rows[:, :, None] == global_slot[None, None, :]
    owner_hot = jnp.any(matches, axis=1)
    page_index = jnp.sum(
        jnp.where(matches, jnp.arange(table_rows.shape[1], dtype=jnp.int32)[None, :, None], 0),
        axis=(0, 1),
    )
    distance = jnp.sum(jnp.where(owner_hot, jnp.arange(SPAN, dtype=jnp.int32)[:, None], 0), axis=0)
    owner_len = jnp.take(lengths, owners)
    slot_len = jnp.sum(jnp.where(owner_hot, owner_len[:, None], 0), axis=0)
    limit = jnp.clip(slot_len - page_index * page_len, 0, page_len)
    wanted = (distance[None, :] == jnp.arange(SPAN, dtype=jnp.int32)[:, None]) & (limit > 0)
    rank = jnp.cumsum(wanted.astype(jnp.int32), axis=1) - 1
    place = wanted[:, :, None] & (rank[:, :, None] == jnp.arange(slots_dev, dtype=jnp.int32))
    order = jnp.sum(jnp.where(place, jnp.arange(slots_dev, dtype=jnp.int32)[None, :, None], 0), axis=1)
    order_limit = jnp.sum(jnp.where(place, limit[None, :, None], 0), axis=1)
    count = jnp.broadcast_to(jnp.sum(wanted.astype(jnp.int32), axis=1, keepdims=True), (SPAN, slots_dev))
    meta = jnp.stack([order, order_limit, count], axis=1).astype(jnp.int32)

    received = [shifted(q_own, "pool", offset) for offset in range(1, SPAN)]
    part_own = attend(0, meta, q_own, cached_key_pages, cached_value_pages, k_new, v_new)
    *received, part_own = lax.optimization_barrier((*received, part_own))
    received = [q_own] + received

    def part(offset):
        return attend(offset, meta, received[offset], cached_key_pages, cached_value_pages)

    stacked = jnp.stack([part_own] + [part(offset) for offset in range(1, SPAN)])
    sums = []
    for start in range(SPAN):
        groups = [
            [(SPAN * k + start + j) % pool_size for j in range(SPAN)]
            for k in range(pool_size // SPAN)
        ]
        mine = lax.dynamic_index_in_dim(stacked, (holder - start) % SPAN, axis=0, keepdims=False)
        sums.append(lax.psum(mine, "pool", axis_index_groups=groups))
    total = lax.dynamic_index_in_dim(jnp.stack(sums), holder % SPAN, axis=0, keepdims=False)
    heads = q_width // HEAD_SIZE
    numerator = total[:rows].reshape(rows, heads, HEAD_SIZE)
    totals = total[rows, : heads * rows].reshape(heads, rows)
    attended = numerator / jnp.transpose(totals)[:, :, None]
    attended = attended.reshape(rows, q_width).astype(jnp.bfloat16)
    return lax.all_to_all(attended, "tensor", split_axis=0, concat_axis=1, tiled=True)


def solution(mesh):
    placed = (
        P(("pool", "tensor"), None),
        P(("pool", "tensor"), None),
        P(("pool", "tensor"), None),
        P("pool", None, "tensor"),
        P("pool", None, "tensor"),
        P(),
        P(),
    )
    return jax.shard_map(
        on_device,
        mesh=mesh,
        in_specs=placed,
        out_specs=P(("pool", "tensor"), None),
        check_vma=False,
    )
```

```python
import functools

import jax
import jax.numpy as jnp
from jax import lax
from jax.experimental import pallas as pl
from jax.experimental.pallas import tpu as pltpu
from jax.sharding import PartitionSpec as P

QUERY_HEADS = 16
KEY_VALUE_HEADS = 8
HEAD_SIZE = 256
SPAN = 4

SOFTCAP = 50.0
SCORE_SCALE = HEAD_SIZE ** (-0.5)


def shifted(block, axis, distance):
    devices = range(lax.axis_size(axis))
    route = [((i - distance) % len(devices), i) for i in devices]
    return lax.ppermute(block, axis, route)


def _attend_kernel(dist, with_own, meta_ref, q_ref, kp_hbm, vp_hbm, *refs):
    if with_own:
        kn_ref, vn_ref = refs[0], refs[1]
        refs = refs[2:]
    out_ref, kbuf, vbuf, sem = refs
    rows = q_ref.shape[0]
    page_len, kv_width = kbuf.shape[1], kbuf.shape[2]
    kv_local = kv_width // HEAD_SIZE
    group = QUERY_HEADS // KEY_VALUE_HEADS
    count = meta_ref[dist, 2, 0]

    def copies(i):
        s = meta_ref[dist, 0, i]
        return (
            pltpu.make_async_copy(kp_hbm.at[s], kbuf.at[i], sem.at[0, i]),
            pltpu.make_async_copy(vp_hbm.at[s], vbuf.at[i], sem.at[1, i]),
        )

    def request(i, carry):
        for c in copies(i):
            c.start()
        return carry

    lax.fori_loop(0, count, request, 0)

    out_ref[...] = jnp.zeros(out_ref.shape, jnp.float32)
    ones = jnp.ones((8, page_len), jnp.bfloat16)

    stacked = [
        jnp.concatenate(
            [q_ref[:, (g * group + a) * HEAD_SIZE:(g * group + a + 1) * HEAD_SIZE] for a in range(group)],
            axis=0,
        )
        for g in range(kv_local)
    ]

    def add_block(k, v, visible):
        for g in range(kv_local):
            kg = k[:, g * HEAD_SIZE:(g + 1) * HEAD_SIZE]
            vg = v[:, g * HEAD_SIZE:(g + 1) * HEAD_SIZE]
            s = lax.dot_general(
                stacked[g], kg, (((1,), (1,)), ((), ())), preferred_element_type=jnp.float32
            ) * SCORE_SCALE
            w = jnp.where(visible, jnp.exp(SOFTCAP * jnp.tanh(s / SOFTCAP)), 0.0).astype(
                jnp.bfloat16
            )
            pv = jnp.dot(w, vg, preferred_element_type=jnp.float32)
            t = lax.dot_general(
                ones, w, (((1,), (1,)), ((), ())), preferred_element_type=jnp.float32
            )
            for a in range(group):
                h = g * group + a
                col = h * HEAD_SIZE
                out_ref[:rows, col:col + HEAD_SIZE] += pv[a * rows:(a + 1) * rows]
            out_ref[rows:rows + 8, g * group * rows:(g + 1) * group * rows] += t

    key_pos = lax.broadcasted_iota(jnp.int32, (group * rows, page_len), 1)
    if with_own:
        q_pos = lax.broadcasted_iota(jnp.int32, (group * rows, page_len), 0) % rows
        add_block(kn_ref[...], vn_ref[...], key_pos <= q_pos)

    def slot(i, carry):
        for c in copies(i):
            c.wait()
        add_block(kbuf[i], vbuf[i], key_pos < meta_ref[dist, 1, i])
        return carry

    lax.fori_loop(0, count, slot, 0)


def attend(dist, meta, q, kp, vp, kn=None, vn=None):
    with_own = kn is not None
    rows, width = q.shape
    slots, page_len, kv_width = kp.shape
    args = [meta, q, kp, vp] + ([kn, vn] if with_own else [])
    blocks = slots // SPAN + (1 if with_own else 0)
    heads = width // HEAD_SIZE
    cost = pl.CostEstimate(
        flops=blocks * heads * rows * page_len * HEAD_SIZE * 4,
        transcendentals=blocks * heads * rows * page_len * 2,
        bytes_accessed=int(q.size) * 2 + blocks * page_len * kv_width * 4
        + (rows + 8) * width * 4,
    )
    vmem = pl.BlockSpec(memory_space=pltpu.VMEM)
    hbm = pl.BlockSpec(memory_space=pl.ANY)
    return pl.pallas_call(
        functools.partial(_attend_kernel, dist, with_own),
        out_shape=jax.ShapeDtypeStruct((rows + 8, width), jnp.float32),
        in_specs=[pl.BlockSpec(memory_space=pltpu.SMEM), vmem, hbm, hbm]
        + [vmem] * (2 if with_own else 0),
        out_specs=vmem,
        scratch_shapes=[
            pltpu.VMEM((slots, page_len, kv_width), kp.dtype),
            pltpu.VMEM((slots, page_len, kv_width), vp.dtype),
            pltpu.SemaphoreType.DMA((2, slots)),
        ],
        cost_estimate=cost,
    )(*args)


def on_device(
    queries,
    incoming_keys,
    incoming_values,
    cached_key_pages,
    cached_value_pages,
    page_table,
    lengths,
):
    tensor_size = lax.axis_size("tensor")
    n_tok = queries.shape[0]
    q_width = queries.shape[1] // tensor_size
    kv_width = incoming_keys.shape[1] // tensor_size
    packed = jnp.concatenate(
        [
            queries.reshape(n_tok, tensor_size, q_width),
            incoming_keys.reshape(n_tok, tensor_size, kv_width),
            incoming_values.reshape(n_tok, tensor_size, kv_width),
        ],
        axis=2,
    )
    mixed = lax.all_to_all(packed, "tensor", split_axis=1, concat_axis=0, tiled=True)
    rows = mixed.shape[0]
    mixed = mixed.reshape(rows, q_width + 2 * kv_width)
    q_own = mixed[:, :q_width]
    k_new = mixed[:, q_width:q_width + kv_width]
    v_new = mixed[:, q_width + kv_width:]

    pool_size = lax.axis_size("pool")
    holder = lax.axis_index("pool")
    slots_dev = cached_key_pages.shape[0]
    page_len = cached_key_pages.shape[1]
    owners = (holder - jnp.arange(SPAN, dtype=jnp.int32)) % pool_size
    table_rows = jnp.take(page_table, owners, axis=0)
    global_slot = holder * slots_dev + jnp.arange(slots_dev, dtype=jnp.int32)
    matches = table_rows[:, :, None] == global_slot[None, None, :]
    owner_hot = jnp.any(matches, axis=1)
    page_index = jnp.sum(
        jnp.where(matches, jnp.arange(table_rows.shape[1], dtype=jnp.int32)[None, :, None], 0),
        axis=(0, 1),
    )
    distance = jnp.sum(jnp.where(owner_hot, jnp.arange(SPAN, dtype=jnp.int32)[:, None], 0), axis=0)
    owner_len = jnp.take(lengths, owners)
    slot_len = jnp.sum(jnp.where(owner_hot, owner_len[:, None], 0), axis=0)
    limit = jnp.clip(slot_len - page_index * page_len, 0, page_len)
    wanted = (distance[None, :] == jnp.arange(SPAN, dtype=jnp.int32)[:, None]) & (limit > 0)
    rank = jnp.cumsum(wanted.astype(jnp.int32), axis=1) - 1
    place = wanted[:, :, None] & (rank[:, :, None] == jnp.arange(slots_dev, dtype=jnp.int32))
    order = jnp.sum(jnp.where(place, jnp.arange(slots_dev, dtype=jnp.int32)[None, :, None], 0), axis=1)
    order_limit = jnp.sum(jnp.where(place, limit[None, :, None], 0), axis=1)
    count = jnp.broadcast_to(jnp.sum(wanted.astype(jnp.int32), axis=1, keepdims=True), (SPAN, slots_dev))
    meta = jnp.stack([order, order_limit, count], axis=1).astype(jnp.int32)

    received = {offset: shifted(q_own, "pool", offset) for offset in range(SPAN - 1, 0, -1)}
    part_own = attend(0, meta, q_own, cached_key_pages, cached_value_pages, k_new, v_new)
    nearer = tuple(received[offset] for offset in range(1, SPAN - 1))
    *nearer, part_own = lax.optimization_barrier((*nearer, part_own))
    received = [q_own] + list(nearer) + [received[SPAN - 1]]

    def part(offset):
        return attend(offset, meta, received[offset], cached_key_pages, cached_value_pages)

    total = part(SPAN - 1)
    for offset in range(SPAN - 2, -1, -1):
        moved = shifted(total, "pool", -1)
        here = part(offset) if offset > 0 else part_own
        moved, here = lax.optimization_barrier((moved, here))
        total = here + moved
    heads = q_width // HEAD_SIZE
    numerator = total[:rows].reshape(rows, heads, HEAD_SIZE)
    totals = total[rows, : heads * rows].reshape(heads, rows)
    attended = numerator / jnp.transpose(totals)[:, :, None]
    attended = attended.reshape(rows, q_width).astype(jnp.bfloat16)
    return lax.all_to_all(attended, "tensor", split_axis=0, concat_axis=1, tiled=True)


def solution(mesh):
    placed = (
        P(("pool", "tensor"), None),
        P(("pool", "tensor"), None),
        P(("pool", "tensor"), None),
        P("pool", None, "tensor"),
        P("pool", None, "tensor"),
        P(),
        P(),
    )
    return jax.shard_map(
        on_device,
        mesh=mesh,
        in_specs=placed,
        out_specs=P(("pool", "tensor"), None),
        check_vma=False,
    )
```

```python
import functools

import jax
import jax.numpy as jnp
from jax import lax
from jax.experimental import pallas as pl
from jax.experimental.pallas import tpu as pltpu
from jax.sharding import PartitionSpec as P

QUERY_HEADS = 16
KEY_VALUE_HEADS = 8
HEAD_SIZE = 256
SPAN = 4

SOFTCAP = 50.0
SCORE_SCALE = HEAD_SIZE ** (-0.5)


def shifted(block, axis, distance):
    devices = range(lax.axis_size(axis))
    route = [((i - distance) % len(devices), i) for i in devices]
    return lax.ppermute(block, axis, route)


def _attend_kernel(dist, with_own, meta_ref, q_ref, kp_hbm, vp_hbm, *refs):
    if with_own:
        kn_ref, vn_ref = refs[0], refs[1]
        refs = refs[2:]
    out_ref, kbuf, vbuf, sem = refs
    rows = q_ref.shape[0]
    page_len, kv_width = kbuf.shape[1], kbuf.shape[2]
    kv_local = kv_width // HEAD_SIZE
    group = QUERY_HEADS // KEY_VALUE_HEADS
    count = meta_ref[dist, 2, 0]

    def copies(i):
        s = meta_ref[dist, 0, i]
        return (
            pltpu.make_async_copy(kp_hbm.at[s], kbuf.at[i], sem.at[0, i]),
            pltpu.make_async_copy(vp_hbm.at[s], vbuf.at[i], sem.at[1, i]),
        )

    def request(i, carry):
        for c in copies(i):
            c.start()
        return carry

    lax.fori_loop(0, count, request, 0)

    out_ref[...] = jnp.zeros(out_ref.shape, jnp.float32)
    ones = jnp.ones((8, page_len), jnp.bfloat16)

    stacked = [
        jnp.concatenate(
            [q_ref[:, (g * group + a) * HEAD_SIZE:(g * group + a + 1) * HEAD_SIZE] for a in range(group)],
            axis=0,
        )
        for g in range(kv_local)
    ]

    def add_block(k, v, visible):
        for g in range(kv_local):
            kg = k[:, g * HEAD_SIZE:(g + 1) * HEAD_SIZE]
            vg = v[:, g * HEAD_SIZE:(g + 1) * HEAD_SIZE]
            s = lax.dot_general(
                stacked[g], kg, (((1,), (1,)), ((), ())), preferred_element_type=jnp.float32
            ) * SCORE_SCALE
            w = jnp.where(visible, jnp.exp(SOFTCAP * jnp.tanh(s / SOFTCAP)), 0.0).astype(
                jnp.bfloat16
            )
            pv = jnp.dot(w, vg, preferred_element_type=jnp.float32)
            t = lax.dot_general(
                ones, w, (((1,), (1,)), ((), ())), preferred_element_type=jnp.float32
            )
            for a in range(group):
                h = g * group + a
                col = h * HEAD_SIZE
                out_ref[:rows, col:col + HEAD_SIZE] += pv[a * rows:(a + 1) * rows]
            out_ref[rows:rows + 8, g * group * rows:(g + 1) * group * rows] += t

    key_pos = lax.broadcasted_iota(jnp.int32, (group * rows, page_len), 1)
    if with_own:
        q_pos = lax.broadcasted_iota(jnp.int32, (group * rows, page_len), 0) % rows
        add_block(kn_ref[...], vn_ref[...], key_pos <= q_pos)

    def slot(i, carry):
        for c in copies(i):
            c.wait()
        add_block(kbuf[i], vbuf[i], key_pos < meta_ref[dist, 1, i])
        return carry

    lax.fori_loop(0, count, slot, 0)


def attend(dist, meta, q, kp, vp, kn=None, vn=None):
    with_own = kn is not None
    rows, width = q.shape
    slots, page_len, kv_width = kp.shape
    args = [meta, q, kp, vp] + ([kn, vn] if with_own else [])
    blocks = slots // SPAN + (1 if with_own else 0)
    heads = width // HEAD_SIZE
    cost = pl.CostEstimate(
        flops=blocks * heads * rows * page_len * HEAD_SIZE * 4,
        transcendentals=blocks * heads * rows * page_len * 2,
        bytes_accessed=int(q.size) * 2 + blocks * page_len * kv_width * 4
        + (rows + 8) * width * 4,
    )
    vmem = pl.BlockSpec(memory_space=pltpu.VMEM)
    hbm = pl.BlockSpec(memory_space=pl.ANY)
    return pl.pallas_call(
        functools.partial(_attend_kernel, dist, with_own),
        out_shape=jax.ShapeDtypeStruct((rows + 8, width), jnp.float32),
        in_specs=[pl.BlockSpec(memory_space=pltpu.SMEM), vmem, hbm, hbm]
        + [vmem] * (2 if with_own else 0),
        out_specs=vmem,
        scratch_shapes=[
            pltpu.VMEM((slots, page_len, kv_width), kp.dtype),
            pltpu.VMEM((slots, page_len, kv_width), vp.dtype),
            pltpu.SemaphoreType.DMA((2, slots)),
        ],
        cost_estimate=cost,
    )(*args)


def on_device(
    queries,
    incoming_keys,
    incoming_values,
    cached_key_pages,
    cached_value_pages,
    page_table,
    lengths,
):
    tensor_size = lax.axis_size("tensor")
    n_tok = queries.shape[0]
    q_width = queries.shape[1] // tensor_size
    kv_width = incoming_keys.shape[1] // tensor_size
    packed = jnp.concatenate(
        [
            queries.reshape(n_tok, tensor_size, q_width),
            incoming_keys.reshape(n_tok, tensor_size, kv_width),
            incoming_values.reshape(n_tok, tensor_size, kv_width),
        ],
        axis=2,
    )
    mixed = lax.all_to_all(packed, "tensor", split_axis=1, concat_axis=0, tiled=True)
    rows = mixed.shape[0]
    mixed = mixed.reshape(rows, q_width + 2 * kv_width)
    q_own = mixed[:, :q_width]
    k_new = mixed[:, q_width:q_width + kv_width]
    v_new = mixed[:, q_width + kv_width:]

    pool_size = lax.axis_size("pool")
    holder = lax.axis_index("pool")
    slots_dev = cached_key_pages.shape[0]
    page_len = cached_key_pages.shape[1]
    owners = (holder - jnp.arange(SPAN, dtype=jnp.int32)) % pool_size
    table_rows = jnp.take(page_table, owners, axis=0)
    global_slot = holder * slots_dev + jnp.arange(slots_dev, dtype=jnp.int32)
    matches = table_rows[:, :, None] == global_slot[None, None, :]
    owner_hot = jnp.any(matches, axis=1)
    page_index = jnp.sum(
        jnp.where(matches, jnp.arange(table_rows.shape[1], dtype=jnp.int32)[None, :, None], 0),
        axis=(0, 1),
    )
    distance = jnp.sum(jnp.where(owner_hot, jnp.arange(SPAN, dtype=jnp.int32)[:, None], 0), axis=0)
    owner_len = jnp.take(lengths, owners)
    slot_len = jnp.sum(jnp.where(owner_hot, owner_len[:, None], 0), axis=0)
    limit = jnp.clip(slot_len - page_index * page_len, 0, page_len)
    wanted = (distance[None, :] == jnp.arange(SPAN, dtype=jnp.int32)[:, None]) & (limit > 0)
    rank = jnp.cumsum(wanted.astype(jnp.int32), axis=1) - 1
    place = wanted[:, :, None] & (rank[:, :, None] == jnp.arange(slots_dev, dtype=jnp.int32))
    order = jnp.sum(jnp.where(place, jnp.arange(slots_dev, dtype=jnp.int32)[None, :, None], 0), axis=1)
    order_limit = jnp.sum(jnp.where(place, limit[None, :, None], 0), axis=1)
    count = jnp.broadcast_to(jnp.sum(wanted.astype(jnp.int32), axis=1, keepdims=True), (SPAN, slots_dev))
    meta = jnp.stack([order, order_limit, count], axis=1).astype(jnp.int32)

    received = [shifted(q_own, "pool", offset) for offset in range(1, SPAN)]
    part_own = attend(0, meta, q_own, cached_key_pages, cached_value_pages, k_new, v_new)
    *received, part_own = lax.optimization_barrier((*received, part_own))
    received = [q_own] + received

    def part(offset):
        return attend(offset, meta, received[offset], cached_key_pages, cached_value_pages)

    total = part(SPAN - 1)
    for offset in range(SPAN - 2, -1, -1):
        here = part(offset) if offset > 0 else part_own
        total, here = lax.optimization_barrier((total, here))
        total = here + shifted(total, "pool", -1)
    heads = q_width // HEAD_SIZE
    numerator = total[:rows].reshape(rows, heads, HEAD_SIZE)
    totals = total[rows, : heads * rows].reshape(heads, rows)
    attended = numerator / jnp.transpose(totals)[:, :, None]
    attended = attended.reshape(rows, q_width).astype(jnp.bfloat16)
    return lax.all_to_all(attended, "tensor", split_axis=0, concat_axis=1, tiled=True)


def solution(mesh):
    placed = (
        P(("pool", "tensor"), None),
        P(("pool", "tensor"), None),
        P(("pool", "tensor"), None),
        P("pool", None, "tensor"),
        P("pool", None, "tensor"),
        P(),
        P(),
    )
    return jax.shard_map(
        on_device,
        mesh=mesh,
        in_specs=placed,
        out_specs=P(("pool", "tensor"), None),
        check_vma=False,
    )
```

```python
import functools

import jax
import jax.numpy as jnp
from jax import lax
from jax.experimental import pallas as pl
from jax.experimental.pallas import tpu as pltpu
from jax.sharding import PartitionSpec as P

QUERY_HEADS = 16
KEY_VALUE_HEADS = 8
HEAD_SIZE = 256
SPAN = 4

SOFTCAP = 50.0
SCORE_SCALE = HEAD_SIZE ** (-0.5)


def shifted(block, axis, distance):
    devices = range(lax.axis_size(axis))
    route = [((i - distance) % len(devices), i) for i in devices]
    return lax.ppermute(block, axis, route)


def _attend_kernel(dist, with_own, meta_ref, q_ref, kp_hbm, vp_hbm, *refs):
    if with_own:
        kn_ref, vn_ref = refs[0], refs[1]
        refs = refs[2:]
    out_ref, kbuf, vbuf, sem = refs
    rows = q_ref.shape[0]
    page_len, kv_width = kbuf.shape[1], kbuf.shape[2]
    kv_local = kv_width // HEAD_SIZE
    group = QUERY_HEADS // KEY_VALUE_HEADS
    count = meta_ref[dist, 2, 0]

    def copies(i):
        s = meta_ref[dist, 0, i]
        return (
            pltpu.make_async_copy(kp_hbm.at[s], kbuf.at[i], sem.at[0, i]),
            pltpu.make_async_copy(vp_hbm.at[s], vbuf.at[i], sem.at[1, i]),
        )

    def request(i, carry):
        for c in copies(i):
            c.start()
        return carry

    lax.fori_loop(0, count, request, 0)

    out_ref[...] = jnp.zeros(out_ref.shape, jnp.float32)
    ones = jnp.ones((8, page_len), jnp.bfloat16)

    stacked = [
        jnp.concatenate(
            [q_ref[:, (g * group + a) * HEAD_SIZE:(g * group + a + 1) * HEAD_SIZE] for a in range(group)],
            axis=0,
        )
        for g in range(kv_local)
    ]

    def add_block(k, v, visible):
        for g in range(kv_local):
            kg = k[:, g * HEAD_SIZE:(g + 1) * HEAD_SIZE]
            vg = v[:, g * HEAD_SIZE:(g + 1) * HEAD_SIZE]
            s = lax.dot_general(
                stacked[g], kg, (((1,), (1,)), ((), ())), preferred_element_type=jnp.float32
            ) * SCORE_SCALE
            w = jnp.where(visible, jnp.exp(SOFTCAP * jnp.tanh(s / SOFTCAP)), 0.0).astype(
                jnp.bfloat16
            )
            pv = jnp.dot(w, vg, preferred_element_type=jnp.float32)
            t = lax.dot_general(
                ones, w, (((1,), (1,)), ((), ())), preferred_element_type=jnp.float32
            )
            for a in range(group):
                h = g * group + a
                col = h * HEAD_SIZE
                out_ref[:rows, col:col + HEAD_SIZE] += pv[a * rows:(a + 1) * rows]
            out_ref[rows:rows + 8, g * group * rows:(g + 1) * group * rows] += t

    key_pos = lax.broadcasted_iota(jnp.int32, (group * rows, page_len), 1)
    if with_own:
        q_pos = lax.broadcasted_iota(jnp.int32, (group * rows, page_len), 0) % rows
        add_block(kn_ref[...], vn_ref[...], key_pos <= q_pos)

    def slot(i, carry):
        for c in copies(i):
            c.wait()
        add_block(kbuf[i], vbuf[i], key_pos < meta_ref[dist, 1, i])
        return carry

    lax.fori_loop(0, count, slot, 0)


def attend(dist, meta, q, kp, vp, kn=None, vn=None):
    with_own = kn is not None
    rows, width = q.shape
    slots, page_len, kv_width = kp.shape
    args = [meta, q, kp, vp] + ([kn, vn] if with_own else [])
    blocks = slots // SPAN + (1 if with_own else 0)
    heads = width // HEAD_SIZE
    cost = pl.CostEstimate(
        flops=blocks * heads * rows * page_len * HEAD_SIZE * 4,
        transcendentals=blocks * heads * rows * page_len * 2,
        bytes_accessed=int(q.size) * 2 + blocks * page_len * kv_width * 4
        + (rows + 8) * width * 4,
    )
    vmem = pl.BlockSpec(memory_space=pltpu.VMEM)
    hbm = pl.BlockSpec(memory_space=pl.ANY)
    return pl.pallas_call(
        functools.partial(_attend_kernel, dist, with_own),
        out_shape=jax.ShapeDtypeStruct((rows + 8, width), jnp.float32),
        in_specs=[pl.BlockSpec(memory_space=pltpu.SMEM), vmem, hbm, hbm]
        + [vmem] * (2 if with_own else 0),
        out_specs=vmem,
        scratch_shapes=[
            pltpu.VMEM((slots, page_len, kv_width), kp.dtype),
            pltpu.VMEM((slots, page_len, kv_width), vp.dtype),
            pltpu.SemaphoreType.DMA((2, slots)),
        ],
        cost_estimate=cost,
    )(*args)


def on_device(
    queries,
    incoming_keys,
    incoming_values,
    cached_key_pages,
    cached_value_pages,
    page_table,
    lengths,
):
    tensor_size = lax.axis_size("tensor")
    n_tok = queries.shape[0]
    q_width = queries.shape[1] // tensor_size
    kv_width = incoming_keys.shape[1] // tensor_size
    packed = jnp.concatenate(
        [
            queries.reshape(n_tok, tensor_size, q_width),
            incoming_keys.reshape(n_tok, tensor_size, kv_width),
            incoming_values.reshape(n_tok, tensor_size, kv_width),
        ],
        axis=2,
    )
    mixed = lax.all_to_all(packed, "tensor", split_axis=1, concat_axis=0, tiled=True)
    rows = mixed.shape[0]
    mixed = mixed.reshape(rows, q_width + 2 * kv_width)
    q_own = mixed[:, :q_width]
    k_new = mixed[:, q_width:q_width + kv_width]
    v_new = mixed[:, q_width + kv_width:]

    pool_size = lax.axis_size("pool")
    holder = lax.axis_index("pool")
    slots_dev = cached_key_pages.shape[0]
    page_len = cached_key_pages.shape[1]
    owners = (holder - jnp.arange(SPAN, dtype=jnp.int32)) % pool_size
    table_rows = jnp.take(page_table, owners, axis=0)
    global_slot = holder * slots_dev + jnp.arange(slots_dev, dtype=jnp.int32)
    matches = table_rows[:, :, None] == global_slot[None, None, :]
    owner_hot = jnp.any(matches, axis=1)
    page_index = jnp.sum(
        jnp.where(matches, jnp.arange(table_rows.shape[1], dtype=jnp.int32)[None, :, None], 0),
        axis=(0, 1),
    )
    distance = jnp.sum(jnp.where(owner_hot, jnp.arange(SPAN, dtype=jnp.int32)[:, None], 0), axis=0)
    owner_len = jnp.take(lengths, owners)
    slot_len = jnp.sum(jnp.where(owner_hot, owner_len[:, None], 0), axis=0)
    limit = jnp.clip(slot_len - page_index * page_len, 0, page_len)
    wanted = (distance[None, :] == jnp.arange(SPAN, dtype=jnp.int32)[:, None]) & (limit > 0)
    rank = jnp.cumsum(wanted.astype(jnp.int32), axis=1) - 1
    place = wanted[:, :, None] & (rank[:, :, None] == jnp.arange(slots_dev, dtype=jnp.int32))
    order = jnp.sum(jnp.where(place, jnp.arange(slots_dev, dtype=jnp.int32)[None, :, None], 0), axis=1)
    order_limit = jnp.sum(jnp.where(place, limit[None, :, None], 0), axis=1)
    count = jnp.broadcast_to(jnp.sum(wanted.astype(jnp.int32), axis=1, keepdims=True), (SPAN, slots_dev))
    meta = jnp.stack([order, order_limit, count], axis=1).astype(jnp.int32)

    received = [shifted(q_own, "pool", offset) for offset in range(SPAN - 1, 0, -1)]
    part_own = attend(0, meta, q_own, cached_key_pages, cached_value_pages, k_new, v_new)
    *received, part_own = lax.optimization_barrier((*received, part_own))
    received = [q_own] + received[::-1]

    def part(offset):
        return attend(offset, meta, received[offset], cached_key_pages, cached_value_pages)

    total = part(SPAN - 1)
    for offset in range(SPAN - 2, -1, -1):
        moved = shifted(total, "pool", -1)
        here = part(offset) if offset > 0 else part_own
        moved, here = lax.optimization_barrier((moved, here))
        total = here + moved
    heads = q_width // HEAD_SIZE
    numerator = total[:rows].reshape(rows, heads, HEAD_SIZE)
    totals = total[rows, : heads * rows].reshape(heads, rows)
    attended = numerator / jnp.transpose(totals)[:, :, None]
    attended = attended.reshape(rows, q_width).astype(jnp.bfloat16)
    return lax.all_to_all(attended, "tensor", split_axis=0, concat_axis=1, tiled=True)


def solution(mesh):
    placed = (
        P(("pool", "tensor"), None),
        P(("pool", "tensor"), None),
        P(("pool", "tensor"), None),
        P("pool", None, "tensor"),
        P("pool", None, "tensor"),
        P(),
        P(),
    )
    return jax.shard_map(
        on_device,
        mesh=mesh,
        in_specs=placed,
        out_specs=P(("pool", "tensor"), None),
        check_vma=False,
    )
```

```python
import functools

import jax
import jax.numpy as jnp
from jax import lax
from jax.experimental import pallas as pl
from jax.experimental.pallas import tpu as pltpu
from jax.sharding import PartitionSpec as P

QUERY_HEADS = 16
KEY_VALUE_HEADS = 8
HEAD_SIZE = 256
SPAN = 4

SOFTCAP = 50.0
SCORE_SCALE = HEAD_SIZE ** (-0.5)


def shifted(block, axis, distance):
    devices = range(lax.axis_size(axis))
    route = [((i - distance) % len(devices), i) for i in devices]
    return lax.ppermute(block, axis, route)


def _attend_kernel(dist, with_own, meta_ref, q_ref, kp_hbm, vp_hbm, *refs):
    if with_own:
        kn_ref, vn_ref = refs[0], refs[1]
        refs = refs[2:]
    out_ref, kbuf, vbuf, sem = refs
    rows = q_ref.shape[0]
    page_len, kv_width = kbuf.shape[1], kbuf.shape[2]
    kv_local = kv_width // HEAD_SIZE
    group = QUERY_HEADS // KEY_VALUE_HEADS
    count = meta_ref[dist, 2, 0]

    def copies(i):
        s = meta_ref[dist, 0, i]
        return (
            pltpu.make_async_copy(kp_hbm.at[s], kbuf.at[i], sem.at[0, i]),
            pltpu.make_async_copy(vp_hbm.at[s], vbuf.at[i], sem.at[1, i]),
        )

    def request(i, carry):
        for c in copies(i):
            c.start()
        return carry

    lax.fori_loop(0, count, request, 0)

    out_ref[...] = jnp.zeros(out_ref.shape, jnp.float32)
    ones = jnp.ones((8, page_len), jnp.bfloat16)

    stacked = [
        jnp.concatenate(
            [q_ref[:, (g * group + a) * HEAD_SIZE:(g * group + a + 1) * HEAD_SIZE] for a in range(group)],
            axis=0,
        )
        for g in range(kv_local)
    ]

    def add_block(k, v, visible):
        for g in range(kv_local):
            kg = k[:, g * HEAD_SIZE:(g + 1) * HEAD_SIZE]
            vg = v[:, g * HEAD_SIZE:(g + 1) * HEAD_SIZE]
            s = lax.dot_general(
                stacked[g], kg, (((1,), (1,)), ((), ())), preferred_element_type=jnp.float32
            ) * SCORE_SCALE
            w = jnp.where(visible, jnp.exp(SOFTCAP * jnp.tanh(s / SOFTCAP)), 0.0).astype(
                jnp.bfloat16
            )
            pv = jnp.dot(w, vg, preferred_element_type=jnp.float32)
            t = lax.dot_general(
                ones, w, (((1,), (1,)), ((), ())), preferred_element_type=jnp.float32
            )
            for a in range(group):
                h = g * group + a
                col = h * HEAD_SIZE
                out_ref[:rows, col:col + HEAD_SIZE] += pv[a * rows:(a + 1) * rows]
            out_ref[rows:rows + 8, g * group * rows:(g + 1) * group * rows] += t

    key_pos = lax.broadcasted_iota(jnp.int32, (group * rows, page_len), 1)
    if with_own:
        q_pos = lax.broadcasted_iota(jnp.int32, (group * rows, page_len), 0) % rows
        add_block(kn_ref[...], vn_ref[...], key_pos <= q_pos)

    def slot(i, carry):
        for c in copies(i):
            c.wait()
        add_block(kbuf[i], vbuf[i], key_pos < meta_ref[dist, 1, i])
        return carry

    lax.fori_loop(0, count, slot, 0)


def attend(dist, meta, q, kp, vp, kn=None, vn=None):
    with_own = kn is not None
    rows, width = q.shape
    slots, page_len, kv_width = kp.shape
    args = [meta, q, kp, vp] + ([kn, vn] if with_own else [])
    blocks = slots // SPAN + (1 if with_own else 0)
    heads = width // HEAD_SIZE
    cost = pl.CostEstimate(
        flops=blocks * heads * rows * page_len * HEAD_SIZE * 4,
        transcendentals=blocks * heads * rows * page_len * 2,
        bytes_accessed=int(q.size) * 2 + blocks * page_len * kv_width * 4
        + (rows + 8) * width * 4,
    )
    vmem = pl.BlockSpec(memory_space=pltpu.VMEM)
    hbm = pl.BlockSpec(memory_space=pl.ANY)
    return pl.pallas_call(
        functools.partial(_attend_kernel, dist, with_own),
        out_shape=jax.ShapeDtypeStruct((rows + 8, width), jnp.float32),
        in_specs=[pl.BlockSpec(memory_space=pltpu.SMEM), vmem, hbm, hbm]
        + [vmem] * (2 if with_own else 0),
        out_specs=vmem,
        scratch_shapes=[
            pltpu.VMEM((slots, page_len, kv_width), kp.dtype),
            pltpu.VMEM((slots, page_len, kv_width), vp.dtype),
            pltpu.SemaphoreType.DMA((2, slots)),
        ],
        cost_estimate=cost,
    )(*args)


def on_device(
    queries,
    incoming_keys,
    incoming_values,
    cached_key_pages,
    cached_value_pages,
    page_table,
    lengths,
):
    tensor_size = lax.axis_size("tensor")
    n_tok = queries.shape[0]
    q_width = queries.shape[1] // tensor_size
    kv_width = incoming_keys.shape[1] // tensor_size
    packed = jnp.concatenate(
        [
            queries.reshape(n_tok, tensor_size, q_width),
            incoming_keys.reshape(n_tok, tensor_size, kv_width),
            incoming_values.reshape(n_tok, tensor_size, kv_width),
        ],
        axis=2,
    )
    mixed = lax.all_to_all(packed, "tensor", split_axis=1, concat_axis=0, tiled=True)
    rows = mixed.shape[0]
    mixed = mixed.reshape(rows, q_width + 2 * kv_width)
    q_own = mixed[:, :q_width]
    k_new = mixed[:, q_width:q_width + kv_width]
    v_new = mixed[:, q_width + kv_width:]

    pool_size = lax.axis_size("pool")
    holder = lax.axis_index("pool")
    slots_dev = cached_key_pages.shape[0]
    page_len = cached_key_pages.shape[1]
    owners = (holder - jnp.arange(SPAN, dtype=jnp.int32)) % pool_size
    table_rows = jnp.take(page_table, owners, axis=0)
    global_slot = holder * slots_dev + jnp.arange(slots_dev, dtype=jnp.int32)
    matches = table_rows[:, :, None] == global_slot[None, None, :]
    owner_hot = jnp.any(matches, axis=1)
    page_index = jnp.sum(
        jnp.where(matches, jnp.arange(table_rows.shape[1], dtype=jnp.int32)[None, :, None], 0),
        axis=(0, 1),
    )
    distance = jnp.sum(jnp.where(owner_hot, jnp.arange(SPAN, dtype=jnp.int32)[:, None], 0), axis=0)
    owner_len = jnp.take(lengths, owners)
    slot_len = jnp.sum(jnp.where(owner_hot, owner_len[:, None], 0), axis=0)
    limit = jnp.clip(slot_len - page_index * page_len, 0, page_len)
    wanted = (distance[None, :] == jnp.arange(SPAN, dtype=jnp.int32)[:, None]) & (limit > 0)
    rank = jnp.cumsum(wanted.astype(jnp.int32), axis=1) - 1
    place = wanted[:, :, None] & (rank[:, :, None] == jnp.arange(slots_dev, dtype=jnp.int32))
    order = jnp.sum(jnp.where(place, jnp.arange(slots_dev, dtype=jnp.int32)[None, :, None], 0), axis=1)
    order_limit = jnp.sum(jnp.where(place, limit[None, :, None], 0), axis=1)
    count = jnp.broadcast_to(jnp.sum(wanted.astype(jnp.int32), axis=1, keepdims=True), (SPAN, slots_dev))
    meta = jnp.stack([order, order_limit, count], axis=1).astype(jnp.int32)

    received = [shifted(q_own, "pool", offset) for offset in range(SPAN - 1, 0, -1)]
    part_own = attend(0, meta, q_own, cached_key_pages, cached_value_pages, k_new, v_new)
    *received, part_own = lax.optimization_barrier((*received, part_own))
    received = [q_own] + received[::-1]

    def part(offset):
        return attend(offset, meta, received[offset], cached_key_pages, cached_value_pages)

    total = part(SPAN - 1)
    for offset in range(SPAN - 2, -1, -1):
        here = part(offset) if offset > 0 else part_own
        total, here = lax.optimization_barrier((total, here))
        total = here + shifted(total, "pool", -1)
    heads = q_width // HEAD_SIZE
    numerator = total[:rows].reshape(rows, heads, HEAD_SIZE)
    totals = total[rows, : heads * rows].reshape(heads, rows)
    attended = numerator / jnp.transpose(totals)[:, :, None]
    attended = attended.reshape(rows, q_width).astype(jnp.bfloat16)
    return lax.all_to_all(attended, "tensor", split_axis=0, concat_axis=1, tiled=True)


def solution(mesh):
    placed = (
        P(("pool", "tensor"), None),
        P(("pool", "tensor"), None),
        P(("pool", "tensor"), None),
        P("pool", None, "tensor"),
        P("pool", None, "tensor"),
        P(),
        P(),
    )
    return jax.shard_map(
        on_device,
        mesh=mesh,
        in_specs=placed,
        out_specs=P(("pool", "tensor"), None),
        check_vma=False,
    )
```
